32 devices in a mesh: groups: 2 (over x), state: 16 (over z, y, core).
Axes of the slice: x: 2, y: 2, z: 4, core: 2. Of those that a mesh axis runs over, the one named last changes fastest.
Arguments:
- forward_probs: float32 [256, 8, 8192], P('groups', None, 'state'), parts along dimension 0, may hold values from 0.1 to 10
- token_ids: int32 [256, 8], P('groups'), parts along dimension 0, may hold values from 0 to 16383
- transition: bfloat16 [8192, 8192], P('state'), may hold values from 0.1 to 10
- emission: bfloat16 [8192, 16384], P('state'), may hold values from 0.05 to 20
Outputs:
- backward_probs: float32 [256, 8, 8192], P('groups', None, 'state'), parts along dimension 0
- trans_counts: float32 [16384, 8192], P(('groups', 'state')), parts along dimension 0
The draws below stay inside these ranges and needn't reach their ends.
There are 2 independent parts, one for each index of `groups`. The reference program is written for one: setup_inputs(seed, part) draws one part's arguments, and reference() takes and returns one part's arrays. A program takes and returns all parts, laid end to end along the dimension named above; an argument that names none is the same for every part. Nothing has to cross between parts.
All inputs are finite; a program needn't handle non-finite values.
Results may differ from the reference program's by a relative error of at most 0.00031.
Values may be sent and summed in bfloat16 or wider, within the bound.
No kernel may reach another device: no remote copies, remote signals or barrier semaphores. Data moves between devices by JAX's collectives and lax.ppermute only.
A program may use at most 192 MiB of HBM per device.

```python
import math
import jax
import jax.numpy as jnp

STATES = 8192
VOCAB = 16384
BATCH = 128
TIME = 8


def draw_transition(key, part):
    blocks = 16
    key_levels, key_noise, key_order = jax.random.split(jax.random.fold_in(key, 11), 3)
    levels = jax.random.uniform(key_levels, (blocks, blocks), jnp.float32, -1.7, 0.3)
    order = jax.random.permutation(key_order, blocks)
    sticky = order[:, None] == jnp.arange(blocks)[None, :]
    levels = jnp.where(sticky, jnp.float32(1.7), levels)
    width = STATES // blocks
    full = jnp.repeat(jnp.repeat(levels, width, axis=0), width, axis=1)
    noise = jax.random.uniform(key_noise, (STATES, STATES), jnp.float32, -0.6, 0.6)
    return jnp.clip(jnp.exp(full + noise), 0.1, 10.0).astype(jnp.bfloat16)


def draw_emission(key, part):
    blocks = 16
    key_levels, key_noise = jax.random.split(jax.random.fold_in(key, 23), 2)
    levels = jax.random.uniform(key_levels, (blocks, blocks), jnp.float32, -2.2, 2.2)
    full = jnp.repeat(jnp.repeat(levels, STATES // blocks, axis=0), VOCAB // blocks, axis=1)
    noise = jax.random.uniform(key_noise, (STATES, VOCAB), jnp.float32, -0.7, 0.7)
    return jnp.clip(jnp.exp(full + noise), 0.05, 20.0).astype(jnp.bfloat16)


def with_ends(entries, own_key, smallest, largest):
    dims = entries.shape
    index_at = [jax.random.randint(jax.random.fold_in(own_key, axis), (), 0, dims[axis]) for axis in range(len(dims))]
    entries = entries.at[tuple(index_at)].set(smallest)
    longest = dims.index(max(dims))
    index_at[longest] = (index_at[longest] + 1) % dims[longest]
    return entries.at[tuple(index_at)].set(largest)


def block_scale(rng, extent, pieces, least, top_value):
    factor_of = 1.0
    for position, blocks in pieces:
        steps = jax.random.uniform(jax.random.fold_in(jax.random.fold_in(rng, 6), position), (blocks,), jnp.float32, least / len(pieces), top_value / len(pieces))
        factor_of = factor_of * jnp.repeat(jnp.exp(steps), extent[position] // blocks).reshape((-1,) + (1,) * (len(extent) - 1 - position))
    return factor_of


def setup_inputs(seed: int = 0, part: int = 0) -> dict:
    streams_of = jax.random.split(jax.random.key(seed), 5)
    own_keys = jax.random.split(jax.random.fold_in(streams_of[4], part), 5)
    forward_probs = jnp.clip(jnp.exp(math.log(10.0) - 4.6051702 * jax.random.uniform(own_keys[0], (BATCH, TIME, STATES), jnp.float32) ** block_scale(own_keys[0], (BATCH, TIME, STATES), ((2, 16),), -0.2, 0.2)), 0.1, 10.0)
    token_ids = with_ends(jax.random.randint(own_keys[1], (BATCH, TIME), 0, VOCAB), jax.random.fold_in(own_keys[1], 1), 0, VOCAB - 1).astype(jnp.int32)
    transition = draw_transition(jax.random.fold_in(streams_of[4], 71), part)
    emission = draw_emission(jax.random.fold_in(streams_of[4], 71), part)
    return {"forward_probs": forward_probs, "token_ids": token_ids, "transition": transition, "emission": emission}


def reference(forward_probs, token_ids, transition, emission):
    emitted = jnp.take(emission, token_ids.reshape(-1), axis=1).astype(jnp.float32)
    emitted = emitted.reshape(STATES, BATCH, TIME)
    backward = jnp.ones((BATCH, STATES), jnp.float32)
    weighted = (emitted[:, :, TIME - 1].T * backward).astype(jnp.bfloat16)
    backs = [backward]
    stored = []
    scales = []
    for t in range(TIME - 2, -1, -1):
        scale_sum = jnp.sum(weighted.astype(jnp.float32), axis=1)
        backward = jnp.dot(weighted, transition.T, preferred_element_type=jnp.float32) / scale_sum[:, None]
        stored.append(weighted)
        scales.append(scale_sum)
        backs.append(backward)
        weighted = (emitted[:, :, t].T * backward).astype(jnp.bfloat16)
    backs = backs[::-1]
    stored = stored[::-1]
    scales = scales[::-1]
    backward_probs = jnp.stack(backs, axis=1)
    shares = []
    for t in range(TIME - 1):
        norm_sum = jnp.sum(forward_probs[:, t, :] * backs[t], axis=1)
        shares.append((forward_probs[:, t, :] / (scales[t] * norm_sum)[:, None]).astype(jnp.bfloat16))
    share_mat = jnp.concatenate(shares, axis=0)
    vector_mat = jnp.concatenate(stored, axis=0)
    moments = jnp.dot(share_mat.T, vector_mat, preferred_element_type=jnp.float32)
    factor = float(STATES) * float(STATES) / float(BATCH * (TIME - 1))
    trans_counts = transition.astype(jnp.float32) * moments * factor
    return backward_probs, trans_counts
```

```python
import jax
import jax.numpy as jnp
from jax import lax
from jax.sharding import PartitionSpec as P


def emitted_rows(token_ids_flat, emission):
    vocab = emission.shape[1]
    onehot = (token_ids_flat[:, None] == lax.broadcasted_iota(jnp.int32, (1, vocab), 1)).astype(emission.dtype)
    return lax.dot_general(
        onehot, emission, (((1,), (1,)), ((), ())), preferred_element_type=jnp.float32
    )


def on_device(forward_probs, token_ids, transition, emission):
    state_rows = transition.shape[0]
    states = transition.shape[1]
    seq_count = token_ids.shape[0]
    step_count = token_ids.shape[1]
    last = step_count - 1
    emitted_last = emitted_rows(token_ids[:, last], emission)
    early_ids = token_ids[:, :last].T.reshape(-1)
    emitted_early = emitted_rows(early_ids, emission).reshape(last, seq_count, state_rows)
    backward = jnp.ones((seq_count, state_rows), jnp.float32)
    weighted = (emitted_last * backward).astype(jnp.bfloat16)
    backs = [backward]
    stored = []
    scales = []
    for t in range(step_count - 2, -1, -1):
        whole = lax.all_gather(weighted, "state", axis=1, tiled=True)
        scale_sum = jnp.sum(whole.astype(jnp.float32), axis=1)
        product = lax.dot_general(
            whole, transition, (((1,), (1,)), ((), ())), preferred_element_type=jnp.float32
        )
        backward = product / scale_sum[:, None]
        stored.append(whole)
        scales.append(scale_sum)
        backs.append(backward)
        if t > 0:
            weighted = (emitted_early[t] * backward).astype(jnp.bfloat16)
    backs = backs[::-1]
    stored = stored[::-1]
    scales = scales[::-1]
    backward_probs = jnp.stack(backs, axis=1)
    partial_norms = jnp.sum(
        forward_probs[:, : step_count - 1, :] * backward_probs[:, : step_count - 1, :], axis=2
    )
    norm_parts = lax.all_gather(partial_norms, "state", axis=0, tiled=False)
    norm_sums = jnp.sum(norm_parts, axis=0)
    shares = []
    for t in range(step_count - 1):
        shares.append(
            (forward_probs[:, t, :] / (scales[t] * norm_sums[:, t])[:, None]).astype(jnp.bfloat16)
        )
    share_mat = jnp.concatenate(shares, axis=0)
    vector_mat = jnp.concatenate(stored, axis=0)
    moments = lax.dot_general(
        share_mat, vector_mat, (((0,), (0,)), ((), ())), preferred_element_type=jnp.float32
    )
    factor = float(states) * float(states) / float(seq_count * (step_count - 1))
    trans_counts = transition.astype(jnp.float32) * moments * factor
    return (backward_probs, trans_counts)


def solution(mesh):
    placed = (P("groups", None, "state"), P("groups", None), P("state", None), P("state", None))
    return jax.shard_map(
        on_device,
        mesh=mesh,
        in_specs=placed,
        out_specs=(P("groups", None, "state"), P(("groups", "state"), None)),
        check_vma=False,
    )
```

```python
import functools

import jax
import jax.numpy as jnp
from jax import lax
from jax.experimental import pallas as pl
from jax.experimental.pallas import tpu as pltpu
from jax.sharding import PartitionSpec as P

NT = (((1,), (1,)), ((), ()))


def _emit_kernel(ids_ref, em_ref, out_ref):
    k = pl.program_id(0)
    tv = em_ref.shape[1]

    @pl.when(k == 0)
    def _():
        out_ref[...] = jnp.zeros_like(out_ref)

    cols = lax.broadcasted_iota(jnp.int32, (ids_ref.shape[0], tv), 1) + k * tv
    onehot = (ids_ref[...] == cols).astype(em_ref.dtype)
    out_ref[...] += lax.dot_general(onehot, em_ref[...], NT, preferred_element_type=jnp.float32)


def emitted_rows(ids, emission, tv=1024):
    n = ids.shape[0]
    rows, vocab = emission.shape
    return pl.pallas_call(
        _emit_kernel,
        grid=(vocab // tv,),
        in_specs=[
            pl.BlockSpec((n, 1), lambda k: (0, 0)),
            pl.BlockSpec((rows, tv), lambda k: (0, k)),
        ],
        out_specs=pl.BlockSpec((n, rows), lambda k: (0, 0)),
        out_shape=jax.ShapeDtypeStruct((n, rows), jnp.float32),
        cost_estimate=pl.CostEstimate(
            flops=2 * n * rows * vocab, bytes_accessed=rows * vocab * 2 + n * rows * 4, transcendentals=0
        ),
    )(ids.reshape(n, 1), emission)


def _step_kernel(whole_ref, trans_ref, emit_ref, fwd_ref, back_ref, wnext_ref, scale_ref, norm_ref, acc_ref, ssum_ref):
    k = pl.program_id(0)

    @pl.when(k == 0)
    def _():
        acc_ref[...] = jnp.zeros_like(acc_ref)
        ssum_ref[...] = jnp.zeros_like(ssum_ref)

    w = whole_ref[...]
    acc_ref[...] += lax.dot_general(w, trans_ref[...], NT, preferred_element_type=jnp.float32)
    ssum_ref[...] += jnp.sum(w.astype(jnp.float32), axis=1, keepdims=True)

    @pl.when(k == pl.num_programs(0) - 1)
    def _():
        s = ssum_ref[...]
        back = acc_ref[...] / s
        back_ref[...] = back
        wnext_ref[...] = (emit_ref[...] * back).astype(wnext_ref.dtype)
        scale_ref[...] = s
        norm_ref[...] = jnp.sum(fwd_ref[...] * back, axis=1, keepdims=True)


def backward_step(whole, transition, emit_next, fwd, tk=2048):
    b, states = whole.shape
    rows = transition.shape[0]
    full = lambda k: (0, 0)
    return pl.pallas_call(
        _step_kernel,
        grid=(states // tk,),
        in_specs=[
            pl.BlockSpec((b, tk), lambda k: (0, k)),
            pl.BlockSpec((rows, tk), lambda k: (0, k)),
            pl.BlockSpec((b, rows), full),
            pl.BlockSpec((b, rows), full),
        ],
        out_specs=[
            pl.BlockSpec((b, rows), full),
            pl.BlockSpec((b, rows), full),
            pl.BlockSpec((b, 1), full),
            pl.BlockSpec((b, 1), full),
        ],
        out_shape=[
            jax.ShapeDtypeStruct((b, rows), jnp.float32),
            jax.ShapeDtypeStruct((b, rows), jnp.bfloat16),
            jax.ShapeDtypeStruct((b, 1), jnp.float32),
            jax.ShapeDtypeStruct((b, 1), jnp.float32),
        ],
        scratch_shapes=[pltpu.VMEM((b, rows), jnp.float32), pltpu.VMEM((b, 1), jnp.float32)],
        cost_estimate=pl.CostEstimate(
            flops=2 * b * rows * states, bytes_accessed=rows * states * 2 + b * states * 2, transcendentals=0
        ),
    )(whole, transition, emit_next, fwd)


def _counts_kernel(factor, steps, share_ref, *refs):
    w_refs = refs[:steps]
    trans_ref = refs[steps]
    out_ref = refs[steps + 1]
    acc = jnp.dot(share_ref[0], w_refs[0][...], preferred_element_type=jnp.float32)
    for t in range(1, steps):
        acc += jnp.dot(share_ref[t], w_refs[t][...], preferred_element_type=jnp.float32)
    out_ref[...] = trans_ref[...].astype(jnp.float32) * acc * factor


def trans_counts_of(share_t, stored, transition, factor, tn=512):
    steps, rows, b = share_t.shape
    states = transition.shape[1]
    return pl.pallas_call(
        functools.partial(_counts_kernel, factor, steps),
        grid=(states // tn,),
        in_specs=[pl.BlockSpec((steps, rows, b), lambda j: (0, 0, 0))]
        + [pl.BlockSpec((b, tn), lambda j: (0, j)) for _ in range(steps)]
        + [pl.BlockSpec((rows, tn), lambda j: (0, j))],
        out_specs=pl.BlockSpec((rows, tn), lambda j: (0, j)),
        out_shape=jax.ShapeDtypeStruct((rows, states), jnp.float32),
        cost_estimate=pl.CostEstimate(
            flops=2 * steps * b * rows * states,
            bytes_accessed=steps * b * states * 2 + rows * states * 6,
            transcendentals=0,
        ),
    )(share_t, *stored, transition)


def on_device(forward_probs, token_ids, transition, emission):
    state_rows = transition.shape[0]
    states = transition.shape[1]
    seq_count = token_ids.shape[0]
    step_count = token_ids.shape[1]
    last = step_count - 1
    emitted_last = emitted_rows(token_ids[:, last], emission)
    early_ids = token_ids[:, :last].T.reshape(-1)
    emitted_early = emitted_rows(early_ids, emission).reshape(last, seq_count, state_rows)
    weighted = emitted_last.astype(jnp.bfloat16)
    backs = [jnp.ones((seq_count, state_rows), jnp.float32)]
    stored = []
    scales = []
    norms = []
    for t in range(step_count - 2, -1, -1):
        whole = lax.all_gather(weighted, "state", axis=1, tiled=True)
        backward, weighted, scale_sum, norm_part = backward_step(
            whole, transition, emitted_early[t], forward_probs[:, t, :]
        )
        stored.append(whole)
        scales.append(scale_sum)
        backs.append(backward)
        norms.append(norm_part)
    backs = backs[::-1]
    stored = stored[::-1]
    scales = jnp.concatenate(scales[::-1], axis=1)
    partial_norms = jnp.concatenate(norms[::-1], axis=1)
    backward_probs = jnp.stack(backs, axis=1)
    norm_parts = lax.all_gather(partial_norms, "state", axis=0, tiled=False)
    norm_sums = jnp.sum(norm_parts, axis=0)
    denom = scales * norm_sums
    share_t = (forward_probs[:, :last, :] / denom[:, :, None]).astype(jnp.bfloat16)
    share_t = jnp.transpose(share_t, (1, 2, 0))
    factor = float(states) * float(states) / float(seq_count * (step_count - 1))
    trans_counts = trans_counts_of(share_t, stored, transition, factor)
    return (backward_probs, trans_counts)


def solution(mesh):
    placed = (P("groups", None, "state"), P("groups", None), P("state", None), P("state", None))
    return jax.shard_map(
        on_device,
        mesh=mesh,
        in_specs=placed,
        out_specs=(P("groups", None, "state"), P(("groups", "state"), None)),
        check_vma=False,
    )
```

```python
import functools

import jax
import jax.numpy as jnp
from jax import lax
from jax.experimental import pallas as pl
from jax.experimental.pallas import tpu as pltpu
from jax.sharding import PartitionSpec as P

NT = (((1,), (1,)), ((), ()))


def _emit_kernel(ids_ref, em_ref, out_ref, acc_ref):
    k = pl.program_id(0)
    tv = em_ref.shape[1]

    @pl.when(k == 0)
    def _():
        acc_ref[...] = jnp.zeros_like(acc_ref)

    cols = lax.broadcasted_iota(jnp.int32, (ids_ref.shape[0], tv), 1) + k * tv
    onehot = (ids_ref[...] == cols).astype(em_ref.dtype)
    acc_ref[...] += lax.dot_general(em_ref[...], onehot, NT, preferred_element_type=jnp.float32)

    @pl.when(k == pl.num_programs(0) - 1)
    def _():
        out_ref[...] = acc_ref[...].T.astype(out_ref.dtype)


def emitted_rows(ids, emission, dtype=jnp.float32, tv=1024):
    n = ids.shape[0]
    rows, vocab = emission.shape
    return pl.pallas_call(
        _emit_kernel,
        grid=(vocab // tv,),
        in_specs=[
            pl.BlockSpec((n, 1), lambda k: (0, 0)),
            pl.BlockSpec((rows, tv), lambda k: (0, k)),
        ],
        out_specs=pl.BlockSpec((n, rows), lambda k: (0, 0)),
        out_shape=jax.ShapeDtypeStruct((n, rows), dtype),
        scratch_shapes=[pltpu.VMEM((rows, n), jnp.float32)],
        cost_estimate=pl.CostEstimate(
            flops=2 * n * rows * vocab, bytes_accessed=rows * vocab * 2 + n * rows * 4, transcendentals=0
        ),
    )(ids.reshape(n, 1), emission)


def _step_kernel(whole_ref, trans_ref, emit_ref, fwd_ref, back_ref, wnext_ref, scale_ref, norm_ref, acc_ref, ssum_ref):
    k = pl.program_id(0)

    @pl.when(k == 0)
    def _():
        acc_ref[...] = jnp.zeros_like(acc_ref)
        ssum_ref[...] = jnp.zeros_like(ssum_ref)

    w = whole_ref[...]
    acc_ref[...] += lax.dot_general(trans_ref[...], w, NT, preferred_element_type=jnp.float32)
    ssum_ref[...] += jnp.sum(w.astype(jnp.float32), axis=1, keepdims=True)

    @pl.when(k == pl.num_programs(0) - 1)
    def _():
        s = ssum_ref[...]
        back = acc_ref[...].T / s
        back_ref[...] = back
        wnext_ref[...] = (emit_ref[...] * back).astype(wnext_ref.dtype)
        scale_ref[...] = s
        norm_ref[...] = jnp.sum(fwd_ref[...] * back, axis=1, keepdims=True)


def backward_step(whole, transition, emit_next, fwd, tk=1024):
    b, states = whole.shape
    rows = transition.shape[0]
    full = lambda k: (0, 0)
    return pl.pallas_call(
        _step_kernel,
        grid=(states // tk,),
        in_specs=[
            pl.BlockSpec((b, tk), lambda k: (0, k)),
            pl.BlockSpec((rows, tk), lambda k: (0, k)),
            pl.BlockSpec((b, rows), full),
            pl.BlockSpec((b, rows), full),
        ],
        out_specs=[
            pl.BlockSpec((b, rows), full),
            pl.BlockSpec((b, rows), full),
            pl.BlockSpec((b, 1), full),
            pl.BlockSpec((b, 1), full),
        ],
        out_shape=[
            jax.ShapeDtypeStruct((b, rows), jnp.float32),
            jax.ShapeDtypeStruct((b, rows), jnp.bfloat16),
            jax.ShapeDtypeStruct((b, 1), jnp.float32),
            jax.ShapeDtypeStruct((b, 1), jnp.float32),
        ],
        scratch_shapes=[pltpu.VMEM((rows, b), jnp.float32), pltpu.VMEM((b, 1), jnp.float32)],
        cost_estimate=pl.CostEstimate(
            flops=2 * b * rows * states, bytes_accessed=rows * states * 2 + b * states * 2, transcendentals=0
        ),
    )(whole, transition, emit_next, fwd)


def _counts_kernel(factor, steps, share_ref, *refs):
    w_refs = refs[:steps]
    trans_ref = refs[steps]
    out_ref = refs[steps + 1]
    cat_ref = refs[steps + 2]
    b = w_refs[0].shape[0]
    for t in range(steps):
        cat_ref[t * b:(t + 1) * b, :] = w_refs[t][...]
    acc = jnp.dot(share_ref[...], cat_ref[...], preferred_element_type=jnp.float32)
    out_ref[...] = trans_ref[...].astype(jnp.float32) * acc * factor


def trans_counts_of(share_cat, stored, transition, factor, tn=512):
    rows, depth = share_cat.shape
    steps = len(stored)
    b = stored[0].shape[0]
    states = transition.shape[1]
    return pl.pallas_call(
        functools.partial(_counts_kernel, factor, steps),
        grid=(states // tn,),
        in_specs=[pl.BlockSpec((rows, depth), lambda j: (0, 0))]
        + [pl.BlockSpec((b, tn), lambda j: (0, j)) for _ in range(steps)]
        + [pl.BlockSpec((rows, tn), lambda j: (0, j))],
        out_specs=pl.BlockSpec((rows, tn), lambda j: (0, j)),
        out_shape=jax.ShapeDtypeStruct((rows, states), jnp.float32),
        scratch_shapes=[pltpu.VMEM((depth, tn), stored[0].dtype)],
        cost_estimate=pl.CostEstimate(
            flops=2 * depth * rows * states,
            bytes_accessed=depth * states * 2 + rows * states * 6,
            transcendentals=0,
        ),
    )(share_cat, *stored, transition)


def on_device(forward_probs, token_ids, transition, emission):
    state_rows = transition.shape[0]
    states = transition.shape[1]
    seq_count = token_ids.shape[0]
    step_count = token_ids.shape[1]
    last = step_count - 1
    emitted_last = emitted_rows(token_ids[:, last], emission, jnp.bfloat16)
    early_ids = token_ids[:, :last].T.reshape(-1)
    emitted_early = emitted_rows(early_ids, emission).reshape(last, seq_count, state_rows)
    weighted = emitted_last
    backs = [jnp.ones((seq_count, state_rows), jnp.float32)]
    stored = []
    scales = []
    norms = []
    for t in range(step_count - 2, -1, -1):
        whole = lax.all_gather(weighted, "state", axis=1, tiled=True)
        backward, weighted, scale_sum, norm_part = backward_step(
            whole, transition, emitted_early[t], forward_probs[:, t, :]
        )
        stored.append(whole)
        scales.append(scale_sum)
        backs.append(backward)
        norms.append(norm_part)
    backs = backs[::-1]
    stored = stored[::-1]
    scales = jnp.concatenate(scales[::-1], axis=1)
    partial_norms = jnp.concatenate(norms[::-1], axis=1)
    backward_probs = jnp.stack(backs, axis=1)
    norm_parts = lax.all_gather(partial_norms, "state", axis=0, tiled=False)
    norm_sums = jnp.sum(norm_parts, axis=0)
    denom = scales * norm_sums
    share_t = (forward_probs[:, :last, :] / denom[:, :, None]).astype(jnp.bfloat16)
    share_cat = jnp.transpose(share_t, (2, 1, 0)).reshape(state_rows, last * seq_count)
    factor = float(states) * float(states) / float(seq_count * (step_count - 1))
    trans_counts = trans_counts_of(share_cat, stored, transition, factor)
    return (backward_probs, trans_counts)


def solution(mesh):
    placed = (P("groups", None, "state"), P("groups", None), P("state", None), P("state", None))
    return jax.shard_map(
        on_device,
        mesh=mesh,
        in_specs=placed,
        out_specs=(P("groups", None, "state"), P(("groups", "state"), None)),
        check_vma=False,
    )
```

```python
import functools

import jax
import jax.numpy as jnp
from jax import lax
from jax.experimental import pallas as pl
from jax.experimental.pallas import tpu as pltpu
from jax.sharding import PartitionSpec as P

NT = (((1,), (1,)), ((), ()))


def _emit_kernel(ids_ref, em_ref, out_ref):
    k = pl.program_id(0)
    tv = em_ref.shape[1]

    @pl.when(k == 0)
    def _():
        out_ref[...] = jnp.zeros_like(out_ref)

    cols = lax.broadcasted_iota(jnp.int32, (ids_ref.shape[0], tv), 1) + k * tv
    onehot = (ids_ref[...] == cols).astype(em_ref.dtype)
    out_ref[...] += lax.dot_general(onehot, em_ref[...], NT, preferred_element_type=jnp.float32)


def emitted_rows(ids, emission, tv=1024):
    n = ids.shape[0]
    rows, vocab = emission.shape
    return pl.pallas_call(
        _emit_kernel,
        grid=(vocab // tv,),
        in_specs=[
            pl.BlockSpec((n, 1), lambda k: (0, 0)),
            pl.BlockSpec((rows, tv), lambda k: (0, k)),
        ],
        out_specs=pl.BlockSpec((n, rows), lambda k: (0, 0)),
        out_shape=jax.ShapeDtypeStruct((n, rows), jnp.float32),
        cost_estimate=pl.CostEstimate(
            flops=2 * n * rows * vocab, bytes_accessed=rows * vocab * 2 + n * rows * 4, transcendentals=0
        ),
    )(ids.reshape(n, 1), emission)


def _step_kernel(whole_ref, trans_ref, emit_ref, fwd_ref, back_ref, wnext_ref, scale_ref, norm_ref, acc_ref, ssum_ref):
    k = pl.program_id(0)

    @pl.when(k == 0)
    def _():
        acc_ref[...] = jnp.zeros_like(acc_ref)
        ssum_ref[...] = jnp.zeros_like(ssum_ref)

    w = whole_ref[...]
    acc_ref[...] += lax.dot_general(w, trans_ref[...], NT, preferred_element_type=jnp.float32)
    ssum_ref[...] += jnp.sum(w.astype(jnp.float32), axis=1, keepdims=True)

    @pl.when(k == pl.num_programs(0) - 1)
    def _():
        s = ssum_ref[...]
        back = acc_ref[...] / s
        back_ref[...] = back
        wnext_ref[...] = (emit_ref[...] * back).astype(wnext_ref.dtype)
        scale_ref[...] = s
        norm_ref[...] = jnp.sum(fwd_ref[...] * back, axis=1, keepdims=True)


def backward_step(whole, transition, emit_next, fwd, tk=2048):
    b, states = whole.shape
    rows = transition.shape[0]
    full = lambda k: (0, 0)
    return pl.pallas_call(
        _step_kernel,
        grid=(states // tk,),
        in_specs=[
            pl.BlockSpec((b, tk), lambda k: (0, k)),
            pl.BlockSpec((rows, tk), lambda k: (0, k)),
            pl.BlockSpec((b, rows), full),
            pl.BlockSpec((b, rows), full),
        ],
        out_specs=[
            pl.BlockSpec((b, rows), full),
            pl.BlockSpec((b, rows), full),
            pl.BlockSpec((b, 1), full),
            pl.BlockSpec((b, 1), full),
        ],
        out_shape=[
            jax.ShapeDtypeStruct((b, rows), jnp.float32),
            jax.ShapeDtypeStruct((b, rows), jnp.bfloat16),
            jax.ShapeDtypeStruct((b, 1), jnp.float32),
            jax.ShapeDtypeStruct((b, 1), jnp.float32),
        ],
        scratch_shapes=[pltpu.VMEM((b, rows), jnp.float32), pltpu.VMEM((b, 1), jnp.float32)],
        cost_estimate=pl.CostEstimate(
            flops=2 * b * rows * states, bytes_accessed=rows * states * 2 + b * states * 2, transcendentals=0
        ),
    )(whole, transition, emit_next, fwd)


def emitted_rows_xla(ids, emission):
    vocab = emission.shape[1]
    onehot = (ids[:, None] == lax.broadcasted_iota(jnp.int32, (1, vocab), 1)).astype(emission.dtype)
    return lax.dot_general(onehot, emission, NT, preferred_element_type=jnp.float32)


def on_device(forward_probs, token_ids, transition, emission):
    state_rows = transition.shape[0]
    states = transition.shape[1]
    seq_count = token_ids.shape[0]
    step_count = token_ids.shape[1]
    last = step_count - 1
    emitted_last = emitted_rows_xla(token_ids[:, last], emission)
    early_ids = token_ids[:, :last].T.reshape(-1)
    emitted_early = emitted_rows(early_ids, emission).reshape(last, seq_count, state_rows)
    weighted = emitted_last.astype(jnp.bfloat16)
    backs = [jnp.ones((seq_count, state_rows), jnp.float32)]
    vector_mat = jnp.zeros((last * seq_count, states), jnp.bfloat16)
    scales = []
    norms = []
    for t in range(step_count - 2, -1, -1):
        whole = lax.all_gather(weighted, "state", axis=1, tiled=True)
        backward, weighted, scale_sum, norm_part = backward_step(
            whole, transition, emitted_early[t], forward_probs[:, t, :]
        )
        vector_mat = lax.dynamic_update_slice(vector_mat, whole, (t * seq_count, 0))
        scales.append(scale_sum)
        backs.append(backward)
        norms.append(norm_part)
    backs = backs[::-1]
    scales = jnp.concatenate(scales[::-1], axis=1)
    partial_norms = jnp.concatenate(norms[::-1], axis=1)
    backward_probs = jnp.stack(backs, axis=1)
    norm_parts = lax.all_gather(partial_norms, "state", axis=0, tiled=False)
    norm_sums = jnp.sum(norm_parts, axis=0)
    denom = scales * norm_sums
    share_t = (forward_probs[:, :last, :] / denom[:, :, None]).astype(jnp.bfloat16)
    share_mat = jnp.transpose(share_t, (1, 0, 2)).reshape(last * seq_count, state_rows)
    moments = lax.dot_general(
        share_mat, vector_mat, (((0,), (0,)), ((), ())), preferred_element_type=jnp.float32
    )
    factor = float(states) * float(states) / float(seq_count * (step_count - 1))
    trans_counts = transition.astype(jnp.float32) * moments * factor
    return (backward_probs, trans_counts)


def solution(mesh):
    placed = (P("groups", None, "state"), P("groups", None), P("state", None), P("state", None))
    return jax.shard_map(
        on_device,
        mesh=mesh,
        in_specs=placed,
        out_specs=(P("groups", None, "state"), P(("groups", "state"), None)),
        check_vma=False,
    )
```

```python
import functools

import jax
import jax.numpy as jnp
from jax import lax
from jax.experimental import pallas as pl
from jax.experimental.pallas import tpu as pltpu
from jax.sharding import PartitionSpec as P

NT = (((1,), (1,)), ((), ()))


def _emit_kernel(ids_ref, em_ref, out_ref):
    k = pl.program_id(0)
    tv = em_ref.shape[1]

    @pl.when(k == 0)
    def _():
        out_ref[...] = jnp.zeros_like(out_ref)

    cols = lax.broadcasted_iota(jnp.int32, (ids_ref.shape[0], tv), 1) + k * tv
    onehot = (ids_ref[...] == cols).astype(em_ref.dtype)
    out_ref[...] += lax.dot_general(onehot, em_ref[...], NT, preferred_element_type=jnp.float32)


def emitted_rows(ids, emission, tv=1024):
    n = ids.shape[0]
    rows, vocab = emission.shape
    return pl.pallas_call(
        _emit_kernel,
        grid=(vocab // tv,),
        in_specs=[
            pl.BlockSpec((n, 1), lambda k: (0, 0)),
            pl.BlockSpec((rows, tv), lambda k: (0, k)),
        ],
        out_specs=pl.BlockSpec((n, rows), lambda k: (0, 0)),
        out_shape=jax.ShapeDtypeStruct((n, rows), jnp.float32),
        cost_estimate=pl.CostEstimate(
            flops=2 * n * rows * vocab, bytes_accessed=rows * vocab * 2 + n * rows * 4, transcendentals=0
        ),
    )(ids.reshape(n, 1), emission)


def _step_kernel(whole_ref, trans_ref, emit_ref, fwd_ref, back_ref, wnext_ref, scale_ref, norm_ref, acc_ref, ssum_ref):
    k = pl.program_id(0)

    @pl.when(k == 0)
    def _():
        acc_ref[...] = jnp.zeros_like(acc_ref)
        ssum_ref[...] = jnp.zeros_like(ssum_ref)

    w = whole_ref[...]
    acc_ref[...] += lax.dot_general(w, trans_ref[...], NT, preferred_element_type=jnp.float32)
    ssum_ref[...] += jnp.sum(w.astype(jnp.float32), axis=1, keepdims=True)

    @pl.when(k == pl.num_programs(0) - 1)
    def _():
        s = ssum_ref[...]
        back = acc_ref[...] / s
        back_ref[...] = back
        wnext_ref[...] = (emit_ref[...] * back).astype(wnext_ref.dtype)
        scale_ref[...] = s
        norm_ref[...] = jnp.sum(fwd_ref[...] * back, axis=1, keepdims=True)


def backward_step(whole, transition, emit_next, fwd, tk=2048):
    b, states = whole.shape
    rows = transition.shape[0]
    full = lambda k: (0, 0)
    return pl.pallas_call(
        _step_kernel,
        grid=(states // tk,),
        in_specs=[
            pl.BlockSpec((b, tk), lambda k: (0, k)),
            pl.BlockSpec((rows, tk), lambda k: (0, k)),
            pl.BlockSpec((b, rows), full),
            pl.BlockSpec((b, rows), full),
        ],
        out_specs=[
            pl.BlockSpec((b, rows), full),
            pl.BlockSpec((b, rows), full),
            pl.BlockSpec((b, 1), full),
            pl.BlockSpec((b, 1), full),
        ],
        out_shape=[
            jax.ShapeDtypeStruct((b, rows), jnp.float32),
            jax.ShapeDtypeStruct((b, rows), jnp.bfloat16),
            jax.ShapeDtypeStruct((b, 1), jnp.float32),
            jax.ShapeDtypeStruct((b, 1), jnp.float32),
        ],
        scratch_shapes=[pltpu.VMEM((b, rows), jnp.float32), pltpu.VMEM((b, 1), jnp.float32)],
        cost_estimate=pl.CostEstimate(
            flops=2 * b * rows * states, bytes_accessed=rows * states * 2 + b * states * 2, transcendentals=0
        ),
    )(whole, transition, emit_next, fwd)


def _transpose_kernel(x_ref, o_ref):
    o_ref[...] = x_ref[...].T


def transposed(x, tile=512):
    rows, cols = x.shape
    return pl.pallas_call(
        _transpose_kernel,
        grid=(cols // tile,),
        in_specs=[pl.BlockSpec((rows, tile), lambda j: (0, j))],
        out_specs=pl.BlockSpec((tile, rows), lambda j: (j, 0)),
        out_shape=jax.ShapeDtypeStruct((cols, rows), x.dtype),
    )(x)


def backward_step_xla(whole, transition_t, emit_next, fwd):
    product = jnp.dot(whole, transition_t, preferred_element_type=jnp.float32)
    scale_sum = jnp.sum(whole.astype(jnp.float32), axis=1, keepdims=True)
    backward = product / scale_sum
    weighted = (emit_next * backward).astype(jnp.bfloat16)
    norm_part = jnp.sum(fwd * backward, axis=1, keepdims=True)
    return backward, weighted, scale_sum, norm_part


def emitted_rows_xla(ids, emission):
    vocab = emission.shape[1]
    onehot = (ids[:, None] == lax.broadcasted_iota(jnp.int32, (1, vocab), 1)).astype(emission.dtype)
    return lax.dot_general(onehot, emission, NT, preferred_element_type=jnp.float32)


def on_device(forward_probs, token_ids, transition, emission):
    state_rows = transition.shape[0]
    states = transition.shape[1]
    seq_count = token_ids.shape[0]
    step_count = token_ids.shape[1]
    last = step_count - 1
    emitted_last = emitted_rows_xla(token_ids[:, last], emission)
    early_ids = token_ids[:, :last].T.reshape(-1)
    emitted_early = emitted_rows(early_ids, emission).reshape(last, seq_count, state_rows)
    weighted = emitted_last.astype(jnp.bfloat16)
    transition_t = transposed(transition)
    backs = [jnp.ones((seq_count, state_rows), jnp.float32)]
    vector_mat = jnp.zeros((last * seq_count, states), jnp.bfloat16)
    scales = []
    norms = []
    for t in range(step_count - 2, -1, -1):
        whole = lax.all_gather(weighted, "state", axis=1, tiled=True)
        backward, weighted, scale_sum, norm_part = backward_step_xla(
            whole, transition_t, emitted_early[t], forward_probs[:, t, :]
        )
        vector_mat = lax.dynamic_update_slice(vector_mat, whole, (t * seq_count, 0))
        scales.append(scale_sum)
        backs.append(backward)
        norms.append(norm_part)
    backs = backs[::-1]
    scales = jnp.concatenate(scales[::-1], axis=1)
    partial_norms = jnp.concatenate(norms[::-1], axis=1)
    backward_probs = jnp.stack(backs, axis=1)
    norm_parts = lax.all_gather(partial_norms, "state", axis=0, tiled=False)
    norm_sums = jnp.sum(norm_parts, axis=0)
    denom = scales * norm_sums
    share_t = (forward_probs[:, :last, :] / denom[:, :, None]).astype(jnp.bfloat16)
    share_mat = jnp.transpose(share_t, (1, 0, 2)).reshape(last * seq_count, state_rows)
    moments = lax.dot_general(
        share_mat, vector_mat, (((0,), (0,)), ((), ())), preferred_element_type=jnp.float32
    )
    factor = float(states) * float(states) / float(seq_count * (step_count - 1))
    trans_counts = transition.astype(jnp.float32) * moments * factor
    return (backward_probs, trans_counts)


def solution(mesh):
    placed = (P("groups", None, "state"), P("groups", None), P("state", None), P("state", None))
    return jax.shard_map(
        on_device,
        mesh=mesh,
        in_specs=placed,
        out_specs=(P("groups", None, "state"), P(("groups", "state"), None)),
        check_vma=False,
    )
```

```python
import functools

import jax
import jax.numpy as jnp
from jax import lax
from jax.experimental import pallas as pl
from jax.experimental.pallas import tpu as pltpu
from jax.sharding import PartitionSpec as P

NT = (((1,), (1,)), ((), ()))


def _emit_kernel(ids_ref, em_ref, out_ref):
    k = pl.program_id(0)
    tv = em_ref.shape[1]

    @pl.when(k == 0)
    def _():
        out_ref[...] = jnp.zeros_like(out_ref)

    cols = lax.broadcasted_iota(jnp.int32, (ids_ref.shape[0], tv), 1) + k * tv
    onehot = (ids_ref[...] == cols).astype(em_ref.dtype)
    out_ref[...] += lax.dot_general(onehot, em_ref[...], NT, preferred_element_type=jnp.float32)


def emitted_rows(ids, emission, tv=1024):
    n = ids.shape[0]
    rows, vocab = emission.shape
    return pl.pallas_call(
        _emit_kernel,
        grid=(vocab // tv,),
        in_specs=[
            pl.BlockSpec((n, 1), lambda k: (0, 0)),
            pl.BlockSpec((rows, tv), lambda k: (0, k)),
        ],
        out_specs=pl.BlockSpec((n, rows), lambda k: (0, 0)),
        out_shape=jax.ShapeDtypeStruct((n, rows), jnp.float32),
        cost_estimate=pl.CostEstimate(
            flops=2 * n * rows * vocab, bytes_accessed=rows * vocab * 2 + n * rows * 4, transcendentals=0
        ),
    )(ids.reshape(n, 1), emission)


def _step_kernel(whole_ref, trans_ref, emit_ref, fwd_ref, back_ref, wnext_ref, scale_ref, norm_ref, acc_ref, ssum_ref):
    k = pl.program_id(0)

    @pl.when(k == 0)
    def _():
        acc_ref[...] = jnp.zeros_like(acc_ref)
        ssum_ref[...] = jnp.zeros_like(ssum_ref)

    w = whole_ref[...]
    acc_ref[...] += lax.dot_general(w, trans_ref[...], NT, preferred_element_type=jnp.float32)
    ssum_ref[...] += jnp.sum(w.astype(jnp.float32), axis=1, keepdims=True)

    @pl.when(k == pl.num_programs(0) - 1)
    def _():
        s = ssum_ref[...]
        back = acc_ref[...] / s
        back_ref[...] = back
        wnext_ref[...] = (emit_ref[...] * back).astype(wnext_ref.dtype)
        scale_ref[...] = s
        norm_ref[...] = jnp.sum(fwd_ref[...] * back, axis=1, keepdims=True)


def backward_step(whole, transition, emit_next, fwd, tk=2048):
    b, states = whole.shape
    rows = transition.shape[0]
    full = lambda k: (0, 0)
    return pl.pallas_call(
        _step_kernel,
        grid=(states // tk,),
        in_specs=[
            pl.BlockSpec((b, tk), lambda k: (0, k)),
            pl.BlockSpec((rows, tk), lambda k: (0, k)),
            pl.BlockSpec((b, rows), full),
            pl.BlockSpec((b, rows), full),
        ],
        out_specs=[
            pl.BlockSpec((b, rows), full),
            pl.BlockSpec((b, rows), full),
            pl.BlockSpec((b, 1), full),
            pl.BlockSpec((b, 1), full),
        ],
        out_shape=[
            jax.ShapeDtypeStruct((b, rows), jnp.float32),
            jax.ShapeDtypeStruct((b, rows), jnp.bfloat16),
            jax.ShapeDtypeStruct((b, 1), jnp.float32),
            jax.ShapeDtypeStruct((b, 1), jnp.float32),
        ],
        scratch_shapes=[pltpu.VMEM((b, rows), jnp.float32), pltpu.VMEM((b, 1), jnp.float32)],
        cost_estimate=pl.CostEstimate(
            flops=2 * b * rows * states, bytes_accessed=rows * states * 2 + b * states * 2, transcendentals=0
        ),
    )(whole, transition, emit_next, fwd)


def _transpose_kernel(x_ref, o_ref):
    o_ref[...] = x_ref[...].T


def transposed(x, tile=512):
    rows, cols = x.shape
    return pl.pallas_call(
        _transpose_kernel,
        grid=(cols // tile,),
        in_specs=[pl.BlockSpec((rows, tile), lambda j: (0, j))],
        out_specs=pl.BlockSpec((tile, rows), lambda j: (j, 0)),
        out_shape=jax.ShapeDtypeStruct((cols, rows), x.dtype),
    )(x)


def with_row_sums(weighted):
    b, rows = weighted.shape
    part = jnp.sum(weighted.astype(jnp.float32), axis=1)
    hi_f32 = lax.reduce_precision(part, exponent_bits=8, mantissa_bits=7)
    hi = hi_f32.astype(jnp.bfloat16)
    lo = (part - hi_f32).astype(jnp.bfloat16)
    extra = jnp.zeros((8, rows), jnp.bfloat16).at[0, :b].set(hi).at[1, :b].set(lo)
    return jnp.concatenate([weighted, extra], axis=0)


def split_gathered(gathered, b, rows):
    whole = gathered[:b]
    hi = gathered[b].reshape(-1, rows)[:, :b].astype(jnp.float32)
    lo = gathered[b + 1].reshape(-1, rows)[:, :b].astype(jnp.float32)
    return whole, jnp.sum(hi + lo, axis=0)[:, None]


def backward_step_xla(whole, scale_sum, transition_t, emit_next, fwd):
    product = jnp.dot(whole, transition_t, preferred_element_type=jnp.float32)
    backward = product / scale_sum
    weighted = (emit_next * backward).astype(jnp.bfloat16)
    norm_part = jnp.sum(fwd * backward, axis=1, keepdims=True)
    return backward, weighted, scale_sum, norm_part


def emitted_rows_xla(ids, emission):
    vocab = emission.shape[1]
    onehot = (ids[:, None] == lax.broadcasted_iota(jnp.int32, (1, vocab), 1)).astype(emission.dtype)
    return lax.dot_general(onehot, emission, NT, preferred_element_type=jnp.float32)


def on_device(forward_probs, token_ids, transition, emission):
    state_rows = transition.shape[0]
    states = transition.shape[1]
    seq_count = token_ids.shape[0]
    step_count = token_ids.shape[1]
    last = step_count - 1
    emitted_last = emitted_rows_xla(token_ids[:, last], emission)
    early_ids = token_ids[:, :last].T.reshape(-1)
    emitted_early = emitted_rows(early_ids, emission).reshape(last, seq_count, state_rows)
    weighted = emitted_last.astype(jnp.bfloat16)
    transition_t = transposed(transition)
    backs = [jnp.ones((seq_count, state_rows), jnp.float32)]
    vector_mat = jnp.zeros((last * seq_count, states), jnp.bfloat16)
    scales = []
    norms = []
    packed = state_rows >= seq_count
    for t in range(step_count - 2, -1, -1):
        if packed:
            gathered = lax.all_gather(with_row_sums(weighted), "state", axis=1, tiled=True)
            whole, scale_sum = split_gathered(gathered, seq_count, state_rows)
        else:
            whole = lax.all_gather(weighted, "state", axis=1, tiled=True)
            scale_sum = jnp.sum(whole.astype(jnp.float32), axis=1, keepdims=True)
        backward, weighted, scale_sum, norm_part = backward_step_xla(
            whole, scale_sum, transition_t, emitted_early[t], forward_probs[:, t, :]
        )
        vector_mat = lax.dynamic_update_slice(vector_mat, whole, (t * seq_count, 0))
        scales.append(scale_sum)
        backs.append(backward)
        norms.append(norm_part)
    backs = backs[::-1]
    scales = jnp.concatenate(scales[::-1], axis=1)
    partial_norms = jnp.concatenate(norms[::-1], axis=1)
    backward_probs = jnp.stack(backs, axis=1)
    norm_parts = lax.all_gather(partial_norms, "state", axis=0, tiled=False)
    norm_sums = jnp.sum(norm_parts, axis=0)
    denom = scales * norm_sums
    share_t = (forward_probs[:, :last, :] / denom[:, :, None]).astype(jnp.bfloat16)
    share_mat = jnp.transpose(share_t, (1, 0, 2)).reshape(last * seq_count, state_rows)
    moments = lax.dot_general(
        share_mat, vector_mat, (((0,), (0,)), ((), ())), preferred_element_type=jnp.float32
    )
    factor = float(states) * float(states) / float(seq_count * (step_count - 1))
    trans_counts = transition.astype(jnp.float32) * moments * factor
    return (backward_probs, trans_counts)


def solution(mesh):
    placed = (P("groups", None, "state"), P("groups", None), P("state", None), P("state", None))
    return jax.shard_map(
        on_device,
        mesh=mesh,
        in_specs=placed,
        out_specs=(P("groups", None, "state"), P(("groups", "state"), None)),
        check_vma=False,
    )
```

```python
import functools

import jax
import jax.numpy as jnp
from jax import lax
from jax.experimental import pallas as pl
from jax.experimental.pallas import tpu as pltpu
from jax.sharding import PartitionSpec as P

NT = (((1,), (1,)), ((), ()))


def _emit_kernel(ids_ref, em_ref, out_ref):
    k = pl.program_id(0)
    tv = em_ref.shape[1]

    @pl.when(k == 0)
    def _():
        out_ref[...] = jnp.zeros_like(out_ref)

    cols = lax.broadcasted_iota(jnp.int32, (ids_ref.shape[0], tv), 1) + k * tv
    onehot = (ids_ref[...] == cols).astype(em_ref.dtype)
    out_ref[...] += lax.dot_general(onehot, em_ref[...], NT, preferred_element_type=jnp.float32)


def emitted_rows(ids, emission, tv=1024):
    n = ids.shape[0]
    rows, vocab = emission.shape
    return pl.pallas_call(
        _emit_kernel,
        grid=(vocab // tv,),
        in_specs=[
            pl.BlockSpec((n, 1), lambda k: (0, 0)),
            pl.BlockSpec((rows, tv), lambda k: (0, k)),
        ],
        out_specs=pl.BlockSpec((n, rows), lambda k: (0, 0)),
        out_shape=jax.ShapeDtypeStruct((n, rows), jnp.float32),
        cost_estimate=pl.CostEstimate(
            flops=2 * n * rows * vocab, bytes_accessed=rows * vocab * 2 + n * rows * 4, transcendentals=0
        ),
    )(ids.reshape(n, 1), emission)


def _step_kernel(whole_ref, trans_ref, emit_ref, fwd_ref, back_ref, wnext_ref, scale_ref, norm_ref, acc_ref, ssum_ref):
    k = pl.program_id(0)

    @pl.when(k == 0)
    def _():
        acc_ref[...] = jnp.zeros_like(acc_ref)
        ssum_ref[...] = jnp.zeros_like(ssum_ref)

    w = whole_ref[...]
    acc_ref[...] += lax.dot_general(w, trans_ref[...], NT, preferred_element_type=jnp.float32)
    ssum_ref[...] += jnp.sum(w.astype(jnp.float32), axis=1, keepdims=True)

    @pl.when(k == pl.num_programs(0) - 1)
    def _():
        s = ssum_ref[...]
        back = acc_ref[...] / s
        back_ref[...] = back
        wnext_ref[...] = (emit_ref[...] * back).astype(wnext_ref.dtype)
        scale_ref[...] = s
        norm_ref[...] = jnp.sum(fwd_ref[...] * back, axis=1, keepdims=True)


def backward_step(whole, transition, emit_next, fwd, tk=2048):
    b, states = whole.shape
    rows = transition.shape[0]
    full = lambda k: (0, 0)
    return pl.pallas_call(
        _step_kernel,
        grid=(states // tk,),
        in_specs=[
            pl.BlockSpec((b, tk), lambda k: (0, k)),
            pl.BlockSpec((rows, tk), lambda k: (0, k)),
            pl.BlockSpec((b, rows), full),
            pl.BlockSpec((b, rows), full),
        ],
        out_specs=[
            pl.BlockSpec((b, rows), full),
            pl.BlockSpec((b, rows), full),
            pl.BlockSpec((b, 1), full),
            pl.BlockSpec((b, 1), full),
        ],
        out_shape=[
            jax.ShapeDtypeStruct((b, rows), jnp.float32),
            jax.ShapeDtypeStruct((b, rows), jnp.bfloat16),
            jax.ShapeDtypeStruct((b, 1), jnp.float32),
            jax.ShapeDtypeStruct((b, 1), jnp.float32),
        ],
        scratch_shapes=[pltpu.VMEM((b, rows), jnp.float32), pltpu.VMEM((b, 1), jnp.float32)],
        cost_estimate=pl.CostEstimate(
            flops=2 * b * rows * states, bytes_accessed=rows * states * 2 + b * states * 2, transcendentals=0
        ),
    )(whole, transition, emit_next, fwd)


def _transpose_kernel(x_ref, o_ref):
    rows = x_ref.shape[0]
    o_ref[:, :rows] = x_ref[...].T
    o_ref[:, rows:] = jnp.ones((o_ref.shape[0], o_ref.shape[1] - rows), o_ref.dtype)


def transposed_with_ones(x, tile=512):
    rows, cols = x.shape
    return pl.pallas_call(
        _transpose_kernel,
        grid=(cols // tile,),
        in_specs=[pl.BlockSpec((rows, tile), lambda j: (0, j))],
        out_specs=pl.BlockSpec((tile, rows + 128), lambda j: (j, 0)),
        out_shape=jax.ShapeDtypeStruct((cols, rows + 128), x.dtype),
    )(x)


def backward_step_xla(whole, transition_t, emit_next, fwd):
    rows = fwd.shape[1]
    product = jnp.dot(whole, transition_t, preferred_element_type=jnp.float32)
    scale_sum = product[:, rows:rows + 1]
    backward = product[:, :rows] / scale_sum
    weighted = (emit_next * backward).astype(jnp.bfloat16)
    norm_part = jnp.sum(fwd * backward, axis=1, keepdims=True)
    return backward, weighted, scale_sum, norm_part


def emitted_rows_xla(ids, emission):
    vocab = emission.shape[1]
    onehot = (ids[:, None] == lax.broadcasted_iota(jnp.int32, (1, vocab), 1)).astype(emission.dtype)
    return lax.dot_general(onehot, emission, NT, preferred_element_type=jnp.float32)


def on_device(forward_probs, token_ids, transition, emission):
    state_rows = transition.shape[0]
    states = transition.shape[1]
    seq_count = token_ids.shape[0]
    step_count = token_ids.shape[1]
    last = step_count - 1
    emitted_last = emitted_rows_xla(token_ids[:, last], emission)
    early_ids = token_ids[:, :last].T.reshape(-1)
    emitted_early = emitted_rows(early_ids, emission).reshape(last, seq_count, state_rows)
    weighted = emitted_last.astype(jnp.bfloat16)
    transition_t = transposed_with_ones(transition)
    backs = [jnp.ones((seq_count, state_rows), jnp.float32)]
    vector_mat = jnp.zeros((last * seq_count, states), jnp.bfloat16)
    scales = []
    norms = []
    for t in range(step_count - 2, -1, -1):
        whole = lax.all_gather(weighted, "state", axis=1, tiled=True)
        backward, weighted, scale_sum, norm_part = backward_step_xla(
            whole, transition_t, emitted_early[t], forward_probs[:, t, :]
        )
        vector_mat = lax.dynamic_update_slice(vector_mat, whole, (t * seq_count, 0))
        scales.append(scale_sum)
        backs.append(backward)
        norms.append(norm_part)
    backs = backs[::-1]
    scales = jnp.concatenate(scales[::-1], axis=1)
    partial_norms = jnp.concatenate(norms[::-1], axis=1)
    backward_probs = jnp.stack(backs, axis=1)
    norm_parts = lax.all_gather(partial_norms, "state", axis=0, tiled=False)
    norm_sums = jnp.sum(norm_parts, axis=0)
    denom = scales * norm_sums
    share_t = (forward_probs[:, :last, :] / denom[:, :, None]).astype(jnp.bfloat16)
    share_mat = jnp.transpose(share_t, (1, 0, 2)).reshape(last * seq_count, state_rows)
    moments = lax.dot_general(
        share_mat, vector_mat, (((0,), (0,)), ((), ())), preferred_element_type=jnp.float32
    )
    factor = float(states) * float(states) / float(seq_count * (step_count - 1))
    trans_counts = transition.astype(jnp.float32) * moments * factor
    return (backward_probs, trans_counts)


def solution(mesh):
    placed = (P("groups", None, "state"), P("groups", None), P("state", None), P("state", None))
    return jax.shard_map(
        on_device,
        mesh=mesh,
        in_specs=placed,
        out_specs=(P("groups", None, "state"), P(("groups", "state"), None)),
        check_vma=False,
    )
```

```python
import functools

import jax
import jax.numpy as jnp
from jax import lax
from jax.experimental import pallas as pl
from jax.experimental.pallas import tpu as pltpu
from jax.sharding import PartitionSpec as P

NT = (((1,), (1,)), ((), ()))


def _emit_kernel(ids_ref, em_ref, out_ref):
    k = pl.program_id(0)
    tv = em_ref.shape[1]

    @pl.when(k == 0)
    def _():
        out_ref[...] = jnp.zeros_like(out_ref)

    cols = lax.broadcasted_iota(jnp.int32, (ids_ref.shape[0], tv), 1) + k * tv
    onehot = (ids_ref[...] == cols).astype(em_ref.dtype)
    out_ref[...] += lax.dot_general(onehot, em_ref[...], NT, preferred_element_type=jnp.float32)


def emitted_rows(ids, emission, tv=1024):
    n = ids.shape[0]
    rows, vocab = emission.shape
    return pl.pallas_call(
        _emit_kernel,
        grid=(vocab // tv,),
        in_specs=[
            pl.BlockSpec((n, 1), lambda k: (0, 0)),
            pl.BlockSpec((rows, tv), lambda k: (0, k)),
        ],
        out_specs=pl.BlockSpec((n, rows), lambda k: (0, 0)),
        out_shape=jax.ShapeDtypeStruct((n, rows), jnp.float32),
        cost_estimate=pl.CostEstimate(
            flops=2 * n * rows * vocab, bytes_accessed=rows * vocab * 2 + n * rows * 4, transcendentals=0
        ),
    )(ids.reshape(n, 1), emission)


def _step_kernel(whole_ref, trans_ref, emit_ref, fwd_ref, back_ref, wnext_ref, scale_ref, norm_ref, acc_ref, ssum_ref):
    k = pl.program_id(0)

    @pl.when(k == 0)
    def _():
        acc_ref[...] = jnp.zeros_like(acc_ref)
        ssum_ref[...] = jnp.zeros_like(ssum_ref)

    w = whole_ref[...]
    acc_ref[...] += lax.dot_general(w, trans_ref[...], NT, preferred_element_type=jnp.float32)
    ssum_ref[...] += jnp.sum(w.astype(jnp.float32), axis=1, keepdims=True)

    @pl.when(k == pl.num_programs(0) - 1)
    def _():
        s = ssum_ref[...]
        back = acc_ref[...] / s
        back_ref[...] = back
        wnext_ref[...] = (emit_ref[...] * back).astype(wnext_ref.dtype)
        scale_ref[...] = s
        norm_ref[...] = jnp.sum(fwd_ref[...] * back, axis=1, keepdims=True)


def backward_step(whole, transition, emit_next, fwd, tk=4096):
    b, states = whole.shape
    rows = transition.shape[0]
    full = lambda k: (0, 0)
    return pl.pallas_call(
        _step_kernel,
        grid=(states // tk,),
        in_specs=[
            pl.BlockSpec((b, tk), lambda k: (0, k)),
            pl.BlockSpec((rows, tk), lambda k: (0, k)),
            pl.BlockSpec((b, rows), full),
            pl.BlockSpec((b, rows), full),
        ],
        out_specs=[
            pl.BlockSpec((b, rows), full),
            pl.BlockSpec((b, rows), full),
            pl.BlockSpec((b, 1), full),
            pl.BlockSpec((b, 1), full),
        ],
        out_shape=[
            jax.ShapeDtypeStruct((b, rows), jnp.float32),
            jax.ShapeDtypeStruct((b, rows), jnp.bfloat16),
            jax.ShapeDtypeStruct((b, 1), jnp.float32),
            jax.ShapeDtypeStruct((b, 1), jnp.float32),
        ],
        scratch_shapes=[pltpu.VMEM((b, rows), jnp.float32), pltpu.VMEM((b, 1), jnp.float32)],
        cost_estimate=pl.CostEstimate(
            flops=2 * b * rows * states, bytes_accessed=rows * states * 2 + b * states * 2, transcendentals=0
        ),
    )(whole, transition, emit_next, fwd)


def emitted_rows_xla(ids, emission):
    vocab = emission.shape[1]
    onehot = (ids[:, None] == lax.broadcasted_iota(jnp.int32, (1, vocab), 1)).astype(emission.dtype)
    return lax.dot_general(onehot, emission, NT, preferred_element_type=jnp.float32)


def on_device(forward_probs, token_ids, transition, emission):
    state_rows = transition.shape[0]
    states = transition.shape[1]
    seq_count = token_ids.shape[0]
    step_count = token_ids.shape[1]
    last = step_count - 1
    emitted_last = emitted_rows_xla(token_ids[:, last], emission)
    early_ids = token_ids[:, :last].T.reshape(-1)
    emitted_early = emitted_rows(early_ids, emission).reshape(last, seq_count, state_rows)
    weighted = emitted_last.astype(jnp.bfloat16)
    backs = [jnp.ones((seq_count, state_rows), jnp.float32)]
    vector_mat = jnp.zeros((last * seq_count, states), jnp.bfloat16)
    scales = []
    norms = []
    for t in range(step_count - 2, -1, -1):
        whole = lax.all_gather(weighted, "state", axis=1, tiled=True)
        backward, weighted, scale_sum, norm_part = backward_step(
            whole, transition, emitted_early[t], forward_probs[:, t, :]
        )
        vector_mat = lax.dynamic_update_slice(vector_mat, whole, (t * seq_count, 0))
        scales.append(scale_sum)
        backs.append(backward)
        norms.append(norm_part)
    backs = backs[::-1]
    scales = jnp.concatenate(scales[::-1], axis=1)
    partial_norms = jnp.concatenate(norms[::-1], axis=1)
    backward_probs = jnp.stack(backs, axis=1)
    norm_parts = lax.all_gather(partial_norms, "state", axis=0, tiled=False)
    norm_sums = jnp.sum(norm_parts, axis=0)
    denom = scales * norm_sums
    share_t = (forward_probs[:, :last, :] / denom[:, :, None]).astype(jnp.bfloat16)
    share_mat = jnp.transpose(share_t, (1, 0, 2)).reshape(last * seq_count, state_rows)
    moments = lax.dot_general(
        share_mat, vector_mat, (((0,), (0,)), ((), ())), preferred_element_type=jnp.float32
    )
    factor = float(states) * float(states) / float(seq_count * (step_count - 1))
    trans_counts = transition.astype(jnp.float32) * moments * factor
    return (backward_probs, trans_counts)


def solution(mesh):
    placed = (P("groups", None, "state"), P("groups", None), P("state", None), P("state", None))
    return jax.shard_map(
        on_device,
        mesh=mesh,
        in_specs=placed,
        out_specs=(P("groups", None, "state"), P(("groups", "state"), None)),
        check_vma=False,
    )
```

```python
import functools

import jax
import jax.numpy as jnp
from jax import lax
from jax.experimental import pallas as pl
from jax.experimental.pallas import tpu as pltpu
from jax.sharding import PartitionSpec as P

NT = (((1,), (1,)), ((), ()))


def _emit_kernel(ids_ref, em_ref, out_ref):
    k = pl.program_id(0)
    tv = em_ref.shape[1]

    @pl.when(k == 0)
    def _():
        out_ref[...] = jnp.zeros_like(out_ref)

    cols = lax.broadcasted_iota(jnp.int32, (ids_ref.shape[0], tv), 1) + k * tv
    onehot = (ids_ref[...] == cols).astype(em_ref.dtype)
    out_ref[...] += lax.dot_general(onehot, em_ref[...], NT, preferred_element_type=jnp.float32)


def emitted_rows(ids, emission, tv=1024):
    n = ids.shape[0]
    rows, vocab = emission.shape
    return pl.pallas_call(
        _emit_kernel,
        grid=(vocab // tv,),
        in_specs=[
            pl.BlockSpec((n, 1), lambda k: (0, 0)),
            pl.BlockSpec((rows, tv), lambda k: (0, k)),
        ],
        out_specs=pl.BlockSpec((n, rows), lambda k: (0, 0)),
        out_shape=jax.ShapeDtypeStruct((n, rows), jnp.float32),
        cost_estimate=pl.CostEstimate(
            flops=2 * n * rows * vocab, bytes_accessed=rows * vocab * 2 + n * rows * 4, transcendentals=0
        ),
    )(ids.reshape(n, 1), emission)


def _step_kernel(whole_ref, trans_ref, emit_ref, fwd_ref, back_ref, wnext_ref, scale_ref, norm_ref, acc_ref, ssum_ref):
    k = pl.program_id(0)

    @pl.when(k == 0)
    def _():
        acc_ref[...] = jnp.zeros_like(acc_ref)
        ssum_ref[...] = jnp.zeros_like(ssum_ref)

    w = whole_ref[...]
    acc_ref[...] += lax.dot_general(w, trans_ref[...], NT, preferred_element_type=jnp.float32)
    ssum_ref[...] += jnp.sum(w.astype(jnp.float32), axis=1, keepdims=True)

    @pl.when(k == pl.num_programs(0) - 1)
    def _():
        s = ssum_ref[...]
        back = acc_ref[...] / s
        back_ref[...] = back
        wnext_ref[...] = (emit_ref[...] * back).astype(wnext_ref.dtype)
        lanes = scale_ref.shape[1]
        scale_ref[...] = jnp.broadcast_to(s, (s.shape[0], lanes))
        norm = jnp.sum(fwd_ref[...] * back, axis=1, keepdims=True)
        norm_ref[...] = jnp.broadcast_to(norm, (norm.shape[0], lanes))


def backward_step(whole, transition, emit_next, fwd, tk=4096):
    b, states = whole.shape
    rows = transition.shape[0]
    full = lambda k: (0, 0)
    return pl.pallas_call(
        _step_kernel,
        grid=(states // tk,),
        in_specs=[
            pl.BlockSpec((b, tk), lambda k: (0, k)),
            pl.BlockSpec((rows, tk), lambda k: (0, k)),
            pl.BlockSpec((b, rows), full),
            pl.BlockSpec((b, rows), full),
        ],
        out_specs=[
            pl.BlockSpec((b, rows), full),
            pl.BlockSpec((b, rows), full),
            pl.BlockSpec((b, 128), full),
            pl.BlockSpec((b, 128), full),
        ],
        out_shape=[
            jax.ShapeDtypeStruct((b, rows), jnp.float32),
            jax.ShapeDtypeStruct((b, rows), jnp.bfloat16),
            jax.ShapeDtypeStruct((b, 128), jnp.float32),
            jax.ShapeDtypeStruct((b, 128), jnp.float32),
        ],
        scratch_shapes=[pltpu.VMEM((b, rows), jnp.float32), pltpu.VMEM((b, 1), jnp.float32)],
        cost_estimate=pl.CostEstimate(
            flops=2 * b * rows * states, bytes_accessed=rows * states * 2 + b * states * 2, transcendentals=0
        ),
    )(whole, transition, emit_next, fwd)


def emitted_rows_xla(ids, emission):
    vocab = emission.shape[1]
    onehot = (ids[:, None] == lax.broadcasted_iota(jnp.int32, (1, vocab), 1)).astype(emission.dtype)
    return lax.dot_general(onehot, emission, NT, preferred_element_type=jnp.float32)


def on_device(forward_probs, token_ids, transition, emission):
    state_rows = transition.shape[0]
    states = transition.shape[1]
    seq_count = token_ids.shape[0]
    step_count = token_ids.shape[1]
    last = step_count - 1
    emitted_last = emitted_rows_xla(token_ids[:, last], emission)
    early_ids = token_ids[:, :last].T.reshape(-1)
    emitted_early = emitted_rows(early_ids, emission).reshape(last, seq_count, state_rows)
    weighted = emitted_last.astype(jnp.bfloat16)
    backs = [jnp.ones((seq_count, state_rows), jnp.float32)]
    vector_mat = jnp.zeros((last * seq_count, states), jnp.bfloat16)
    scales = []
    norms = []
    for t in range(step_count - 2, -1, -1):
        whole = lax.all_gather(weighted, "state", axis=1, tiled=True)
        backward, weighted, scale_sum, norm_part = backward_step(
            whole, transition, emitted_early[t], forward_probs[:, t, :]
        )
        vector_mat = lax.dynamic_update_slice(vector_mat, whole, (t * seq_count, 0))
        scales.append(scale_sum[:, :1])
        backs.append(backward)
        norms.append(norm_part[:, :1])
    backs = backs[::-1]
    scales = jnp.concatenate(scales[::-1], axis=1)
    partial_norms = jnp.concatenate(norms[::-1], axis=1)
    backward_probs = jnp.stack(backs, axis=1)
    norm_parts = lax.all_gather(partial_norms, "state", axis=0, tiled=False)
    norm_sums = jnp.sum(norm_parts, axis=0)
    denom = scales * norm_sums
    share_t = (forward_probs[:, :last, :] / denom[:, :, None]).astype(jnp.bfloat16)
    share_mat = jnp.transpose(share_t, (1, 0, 2)).reshape(last * seq_count, state_rows)
    moments = lax.dot_general(
        share_mat, vector_mat, (((0,), (0,)), ((), ())), preferred_element_type=jnp.float32
    )
    factor = float(states) * float(states) / float(seq_count * (step_count - 1))
    trans_counts = transition.astype(jnp.float32) * moments * factor
    return (backward_probs, trans_counts)


def solution(mesh):
    placed = (P("groups", None, "state"), P("groups", None), P("state", None), P("state", None))
    return jax.shard_map(
        on_device,
        mesh=mesh,
        in_specs=placed,
        out_specs=(P("groups", None, "state"), P(("groups", "state"), None)),
        check_vma=False,
    )
```

```python
import functools

import jax
import jax.numpy as jnp
from jax import lax
from jax.experimental import pallas as pl
from jax.experimental.pallas import tpu as pltpu
from jax.sharding import PartitionSpec as P

NT = (((1,), (1,)), ((), ()))


def _emit_kernel(ids_ref, em_ref, out_ref):
    k = pl.program_id(0)
    tv = em_ref.shape[1]

    @pl.when(k == 0)
    def _():
        out_ref[...] = jnp.zeros_like(out_ref)

    cols = lax.broadcasted_iota(jnp.int32, (ids_ref.shape[0], tv), 1) + k * tv
    onehot = (ids_ref[...] == cols).astype(em_ref.dtype)
    out_ref[...] += lax.dot_general(onehot, em_ref[...], NT, preferred_element_type=jnp.float32)


def emitted_rows(ids, emission, tv=1024):
    n = ids.shape[0]
    rows, vocab = emission.shape
    return pl.pallas_call(
        _emit_kernel,
        grid=(vocab // tv,),
        in_specs=[
            pl.BlockSpec((n, 1), lambda k: (0, 0)),
            pl.BlockSpec((rows, tv), lambda k: (0, k)),
        ],
        out_specs=pl.BlockSpec((n, rows), lambda k: (0, 0)),
        out_shape=jax.ShapeDtypeStruct((n, rows), jnp.float32),
        cost_estimate=pl.CostEstimate(
            flops=2 * n * rows * vocab, bytes_accessed=rows * vocab * 2 + n * rows * 4, transcendentals=0
        ),
    )(ids.reshape(n, 1), emission)


def _step_kernel(whole_ref, trans_ref, emit_ref, fwd_ref, back_ref, wnext_ref, scale_ref, norm_ref, acc_ref, ssum_ref):
    k = pl.program_id(0)

    @pl.when(k == 0)
    def _():
        acc_ref[...] = jnp.zeros_like(acc_ref)
        ssum_ref[...] = jnp.zeros_like(ssum_ref)

    w = whole_ref[...]
    acc_ref[...] += jnp.dot(w, trans_ref[...], preferred_element_type=jnp.float32)
    ssum_ref[...] += jnp.sum(w.astype(jnp.float32), axis=1, keepdims=True)

    @pl.when(k == pl.num_programs(0) - 1)
    def _():
        s = ssum_ref[...]
        back = acc_ref[...] / s
        back_ref[...] = back
        wnext_ref[...] = (emit_ref[...] * back).astype(wnext_ref.dtype)
        scale_ref[...] = s
        norm_ref[...] = jnp.sum(fwd_ref[...] * back, axis=1, keepdims=True)


def backward_step(whole, transition_t, emit_next, fwd, tk=4096):
    b, states = whole.shape
    rows = transition_t.shape[1]
    full = lambda k: (0, 0)
    return pl.pallas_call(
        _step_kernel,
        grid=(states // tk,),
        in_specs=[
            pl.BlockSpec((b, tk), lambda k: (0, k)),
            pl.BlockSpec((tk, rows), lambda k: (k, 0)),
            pl.BlockSpec((b, rows), full),
            pl.BlockSpec((b, rows), full),
        ],
        out_specs=[
            pl.BlockSpec((b, rows), full),
            pl.BlockSpec((b, rows), full),
            pl.BlockSpec((b, 1), full),
            pl.BlockSpec((b, 1), full),
        ],
        out_shape=[
            jax.ShapeDtypeStruct((b, rows), jnp.float32),
            jax.ShapeDtypeStruct((b, rows), jnp.bfloat16),
            jax.ShapeDtypeStruct((b, 1), jnp.float32),
            jax.ShapeDtypeStruct((b, 1), jnp.float32),
        ],
        scratch_shapes=[pltpu.VMEM((b, rows), jnp.float32), pltpu.VMEM((b, 1), jnp.float32)],
        cost_estimate=pl.CostEstimate(
            flops=2 * b * rows * states, bytes_accessed=rows * states * 2 + b * states * 2, transcendentals=0
        ),
    )(whole, transition_t, emit_next, fwd)


def _transpose_kernel(x_ref, o_ref):
    o_ref[...] = x_ref[...].T


def transposed(x, tile=512):
    rows, cols = x.shape
    return pl.pallas_call(
        _transpose_kernel,
        grid=(cols // tile,),
        in_specs=[pl.BlockSpec((rows, tile), lambda j: (0, j))],
        out_specs=pl.BlockSpec((tile, rows), lambda j: (j, 0)),
        out_shape=jax.ShapeDtypeStruct((cols, rows), x.dtype),
    )(x)


def emitted_rows_xla(ids, emission):
    vocab = emission.shape[1]
    onehot = (ids[:, None] == lax.broadcasted_iota(jnp.int32, (1, vocab), 1)).astype(emission.dtype)
    return lax.dot_general(onehot, emission, NT, preferred_element_type=jnp.float32)


def on_device(forward_probs, token_ids, transition, emission):
    state_rows = transition.shape[0]
    states = transition.shape[1]
    seq_count = token_ids.shape[0]
    step_count = token_ids.shape[1]
    last = step_count - 1
    emitted_last = emitted_rows_xla(token_ids[:, last], emission)
    early_ids = token_ids[:, :last].T.reshape(-1)
    emitted_early = emitted_rows(early_ids, emission).reshape(last, seq_count, state_rows)
    weighted = emitted_last.astype(jnp.bfloat16)
    transition_t = transposed(transition)
    backs = [jnp.ones((seq_count, state_rows), jnp.float32)]
    vector_mat = jnp.zeros((last * seq_count, states), jnp.bfloat16)
    scales = []
    norms = []
    for t in range(step_count - 2, -1, -1):
        whole = lax.all_gather(weighted, "state", axis=1, tiled=True)
        backward, weighted, scale_sum, norm_part = backward_step(
            whole, transition_t, emitted_early[t], forward_probs[:, t, :]
        )
        vector_mat = lax.dynamic_update_slice(vector_mat, whole, (t * seq_count, 0))
        scales.append(scale_sum)
        backs.append(backward)
        norms.append(norm_part)
    backs = backs[::-1]
    scales = jnp.concatenate(scales[::-1], axis=1)
    partial_norms = jnp.concatenate(norms[::-1], axis=1)
    backward_probs = jnp.stack(backs, axis=1)
    norm_parts = lax.all_gather(partial_norms, "state", axis=0, tiled=False)
    norm_sums = jnp.sum(norm_parts, axis=0)
    denom = scales * norm_sums
    share_t = (forward_probs[:, :last, :] / denom[:, :, None]).astype(jnp.bfloat16)
    share_mat = jnp.transpose(share_t, (1, 0, 2)).reshape(last * seq_count, state_rows)
    moments = lax.dot_general(
        share_mat, vector_mat, (((0,), (0,)), ((), ())), preferred_element_type=jnp.float32
    )
    factor = float(states) * float(states) / float(seq_count * (step_count - 1))
    trans_counts = transition.astype(jnp.float32) * moments * factor
    return (backward_probs, trans_counts)


def solution(mesh):
    placed = (P("groups", None, "state"), P("groups", None), P("state", None), P("state", None))
    return jax.shard_map(
        on_device,
        mesh=mesh,
        in_specs=placed,
        out_specs=(P("groups", None, "state"), P(("groups", "state"), None)),
        check_vma=False,
    )
```

```python
import functools

import jax
import jax.numpy as jnp
from jax import lax
from jax.experimental import pallas as pl
from jax.experimental.pallas import tpu as pltpu
from jax.sharding import PartitionSpec as P

NT = (((1,), (1,)), ((), ()))


def _emit_kernel(ids_ref, em_ref, out_ref):
    k = pl.program_id(0)
    tv = em_ref.shape[1]

    @pl.when(k == 0)
    def _():
        out_ref[...] = jnp.zeros_like(out_ref)

    cols = lax.broadcasted_iota(jnp.int32, (ids_ref.shape[0], tv), 1) + k * tv
    onehot = (ids_ref[...] == cols).astype(em_ref.dtype)
    out_ref[...] += lax.dot_general(onehot, em_ref[...], NT, preferred_element_type=jnp.float32)


def emitted_rows(ids, emission, tv=1024):
    n = ids.shape[0]
    rows, vocab = emission.shape
    return pl.pallas_call(
        _emit_kernel,
        grid=(vocab // tv,),
        in_specs=[
            pl.BlockSpec((n, 1), lambda k: (0, 0)),
            pl.BlockSpec((rows, tv), lambda k: (0, k)),
        ],
        out_specs=pl.BlockSpec((n, rows), lambda k: (0, 0)),
        out_shape=jax.ShapeDtypeStruct((n, rows), jnp.float32),
        cost_estimate=pl.CostEstimate(
            flops=2 * n * rows * vocab, bytes_accessed=rows * vocab * 2 + n * rows * 4, transcendentals=0
        ),
    )(ids.reshape(n, 1), emission)


def _step_kernel(whole_ref, trans_ref, emit_ref, fwd_ref, back_ref, wnext_ref, scale_ref, norm_ref, acc_ref, ssum_ref):
    k = pl.program_id(0)

    @pl.when(k == 0)
    def _():
        acc_ref[...] = jnp.zeros_like(acc_ref)
        ssum_ref[...] = jnp.zeros_like(ssum_ref)

    w = whole_ref[...]
    acc_ref[...] += jnp.dot(w, trans_ref[...], preferred_element_type=jnp.float32)
    ssum_ref[...] += jnp.sum(w.astype(jnp.float32), axis=1, keepdims=True)

    @pl.when(k == pl.num_programs(0) - 1)
    def _():
        s = ssum_ref[...]
        back = acc_ref[...] / s
        back_ref[...] = back
        wnext_ref[...] = (emit_ref[...] * back).astype(wnext_ref.dtype)
        scale_ref[...] = s
        norm_ref[...] = jnp.sum(fwd_ref[...] * back, axis=1, keepdims=True)


def backward_step(whole, transition_t, emit_next, fwd, tk=2048):
    b, states = whole.shape
    rows = transition_t.shape[1]
    full = lambda k: (0, 0)
    return pl.pallas_call(
        _step_kernel,
        grid=(states // tk,),
        in_specs=[
            pl.BlockSpec((b, tk), lambda k: (0, k)),
            pl.BlockSpec((tk, rows), lambda k: (k, 0)),
            pl.BlockSpec((b, rows), full),
            pl.BlockSpec((b, rows), full),
        ],
        out_specs=[
            pl.BlockSpec((b, rows), full),
            pl.BlockSpec((b, rows), full),
            pl.BlockSpec((b, 1), full),
            pl.BlockSpec((b, 1), full),
        ],
        out_shape=[
            jax.ShapeDtypeStruct((b, rows), jnp.float32),
            jax.ShapeDtypeStruct((b, rows), jnp.bfloat16),
            jax.ShapeDtypeStruct((b, 1), jnp.float32),
            jax.ShapeDtypeStruct((b, 1), jnp.float32),
        ],
        scratch_shapes=[pltpu.VMEM((b, rows), jnp.float32), pltpu.VMEM((b, 1), jnp.float32)],
        cost_estimate=pl.CostEstimate(
            flops=2 * b * rows * states, bytes_accessed=rows * states * 2 + b * states * 2, transcendentals=0
        ),
    )(whole, transition_t, emit_next, fwd)


def _transpose_kernel(x_ref, o_ref):
    o_ref[...] = x_ref[...].T


def transposed(x, tile=512):
    rows, cols = x.shape
    return pl.pallas_call(
        _transpose_kernel,
        grid=(cols // tile,),
        in_specs=[pl.BlockSpec((rows, tile), lambda j: (0, j))],
        out_specs=pl.BlockSpec((tile, rows), lambda j: (j, 0)),
        out_shape=jax.ShapeDtypeStruct((cols, rows), x.dtype),
    )(x)


def emitted_rows_xla(ids, emission):
    vocab = emission.shape[1]
    onehot = (ids[:, None] == lax.broadcasted_iota(jnp.int32, (1, vocab), 1)).astype(emission.dtype)
    return lax.dot_general(onehot, emission, NT, preferred_element_type=jnp.float32)


def on_device(forward_probs, token_ids, transition, emission):
    state_rows = transition.shape[0]
    states = transition.shape[1]
    seq_count = token_ids.shape[0]
    step_count = token_ids.shape[1]
    last = step_count - 1
    emitted_last = emitted_rows_xla(token_ids[:, last], emission)
    early_ids = token_ids[:, :last].T.reshape(-1)
    emitted_early = emitted_rows(early_ids, emission).reshape(last, seq_count, state_rows)
    weighted = emitted_last.astype(jnp.bfloat16)
    transition_t = transposed(transition)
    backs = [jnp.ones((seq_count, state_rows), jnp.float32)]
    vector_mat = jnp.zeros((last * seq_count, states), jnp.bfloat16)
    scales = []
    norms = []
    for t in range(step_count - 2, -1, -1):
        whole = lax.all_gather(weighted, "state", axis=1, tiled=True)
        backward, weighted, scale_sum, norm_part = backward_step(
            whole, transition_t, emitted_early[t], forward_probs[:, t, :]
        )
        vector_mat = lax.dynamic_update_slice(vector_mat, whole, (t * seq_count, 0))
        scales.append(scale_sum)
        backs.append(backward)
        norms.append(norm_part)
    backs = backs[::-1]
    scales = jnp.concatenate(scales[::-1], axis=1)
    partial_norms = jnp.concatenate(norms[::-1], axis=1)
    backward_probs = jnp.stack(backs, axis=1)
    norm_parts = lax.all_gather(partial_norms, "state", axis=0, tiled=False)
    norm_sums = jnp.sum(norm_parts, axis=0)
    denom = scales * norm_sums
    share_t = (forward_probs[:, :last, :] / denom[:, :, None]).astype(jnp.bfloat16)
    share_mat = jnp.transpose(share_t, (1, 0, 2)).reshape(last * seq_count, state_rows)
    moments = lax.dot_general(
        share_mat, vector_mat, (((0,), (0,)), ((), ())), preferred_element_type=jnp.float32
    )
    factor = float(states) * float(states) / float(seq_count * (step_count - 1))
    trans_counts = transition.astype(jnp.float32) * moments * factor
    return (backward_probs, trans_counts)


def solution(mesh):
    placed = (P("groups", None, "state"), P("groups", None), P("state", None), P("state", None))
    return jax.shard_map(
        on_device,
        mesh=mesh,
        in_specs=placed,
        out_specs=(P("groups", None, "state"), P(("groups", "state"), None)),
        check_vma=False,
    )
```

```python
import functools

import jax
import jax.numpy as jnp
from jax import lax
from jax.experimental import pallas as pl
from jax.experimental.pallas import tpu as pltpu
from jax.sharding import PartitionSpec as P

NT = (((1,), (1,)), ((), ()))


def _emit_kernel(ids_ref, em_ref, out_ref):
    k = pl.program_id(0)
    tv = em_ref.shape[1]

    @pl.when(k == 0)
    def _():
        out_ref[...] = jnp.zeros_like(out_ref)

    cols = lax.broadcasted_iota(jnp.int32, (ids_ref.shape[0], tv), 1) + k * tv
    onehot = (ids_ref[...] == cols).astype(em_ref.dtype)
    out_ref[...] += lax.dot_general(onehot, em_ref[...], NT, preferred_element_type=jnp.float32)


def emitted_rows(ids, emission, tv=1024):
    n = ids.shape[0]
    rows, vocab = emission.shape
    return pl.pallas_call(
        _emit_kernel,
        grid=(vocab // tv,),
        in_specs=[
            pl.BlockSpec((n, 1), lambda k: (0, 0)),
            pl.BlockSpec((rows, tv), lambda k: (0, k)),
        ],
        out_specs=pl.BlockSpec((n, rows), lambda k: (0, 0)),
        out_shape=jax.ShapeDtypeStruct((n, rows), jnp.float32),
        cost_estimate=pl.CostEstimate(
            flops=2 * n * rows * vocab, bytes_accessed=rows * vocab * 2 + n * rows * 4, transcendentals=0
        ),
    )(ids.reshape(n, 1), emission)


def _step_kernel(whole_ref, trans_ref, emit_ref, fwd_ref, back_ref, wnext_ref, scale_ref, norm_ref, acc_ref, ssum_ref):
    k = pl.program_id(0)

    @pl.when(k == 0)
    def _():
        acc_ref[...] = jnp.zeros_like(acc_ref)
        ssum_ref[...] = jnp.zeros_like(ssum_ref)

    w = whole_ref[...]
    acc_ref[...] += jnp.dot(w, trans_ref[...], preferred_element_type=jnp.float32)
    ssum_ref[...] += jnp.sum(w.astype(jnp.float32), axis=1, keepdims=True)

    @pl.when(k == pl.num_programs(0) - 1)
    def _():
        s = ssum_ref[...]
        back = acc_ref[...] / s
        back_ref[...] = back
        wnext_ref[...] = (emit_ref[...] * back).astype(wnext_ref.dtype)
        scale_ref[...] = s
        norm_ref[...] = jnp.sum(fwd_ref[...] * back, axis=1, keepdims=True)


def backward_step(whole, transition_t, emit_next, fwd, tk=8192):
    b, states = whole.shape
    rows = transition_t.shape[1]
    full = lambda k: (0, 0)
    return pl.pallas_call(
        _step_kernel,
        grid=(states // tk,),
        in_specs=[
            pl.BlockSpec((b, tk), lambda k: (0, k)),
            pl.BlockSpec((tk, rows), lambda k: (k, 0)),
            pl.BlockSpec((b, rows), full),
            pl.BlockSpec((b, rows), full),
        ],
        out_specs=[
            pl.BlockSpec((b, rows), full),
            pl.BlockSpec((b, rows), full),
            pl.BlockSpec((b, 1), full),
            pl.BlockSpec((b, 1), full),
        ],
        out_shape=[
            jax.ShapeDtypeStruct((b, rows), jnp.float32),
            jax.ShapeDtypeStruct((b, rows), jnp.bfloat16),
            jax.ShapeDtypeStruct((b, 1), jnp.float32),
            jax.ShapeDtypeStruct((b, 1), jnp.float32),
        ],
        scratch_shapes=[pltpu.VMEM((b, rows), jnp.float32), pltpu.VMEM((b, 1), jnp.float32)],
        cost_estimate=pl.CostEstimate(
            flops=2 * b * rows * states, bytes_accessed=rows * states * 2 + b * states * 2, transcendentals=0
        ),
    )(whole, transition_t, emit_next, fwd)


def _transpose_kernel(x_ref, o_ref):
    o_ref[...] = x_ref[...].T


def transposed(x, tile=512):
    rows, cols = x.shape
    return pl.pallas_call(
        _transpose_kernel,
        grid=(cols // tile,),
        in_specs=[pl.BlockSpec((rows, tile), lambda j: (0, j))],
        out_specs=pl.BlockSpec((tile, rows), lambda j: (j, 0)),
        out_shape=jax.ShapeDtypeStruct((cols, rows), x.dtype),
    )(x)


def emitted_rows_xla(ids, emission):
    vocab = emission.shape[1]
    onehot = (ids[:, None] == lax.broadcasted_iota(jnp.int32, (1, vocab), 1)).astype(emission.dtype)
    return lax.dot_general(onehot, emission, NT, preferred_element_type=jnp.float32)


def on_device(forward_probs, token_ids, transition, emission):
    state_rows = transition.shape[0]
    states = transition.shape[1]
    seq_count = token_ids.shape[0]
    step_count = token_ids.shape[1]
    last = step_count - 1
    emitted_last = emitted_rows_xla(token_ids[:, last], emission)
    early_ids = token_ids[:, :last].T.reshape(-1)
    emitted_early = emitted_rows(early_ids, emission).reshape(last, seq_count, state_rows)
    weighted = emitted_last.astype(jnp.bfloat16)
    transition_t = transposed(transition)
    backs = [jnp.ones((seq_count, state_rows), jnp.float32)]
    vector_mat = jnp.zeros((last * seq_count, states), jnp.bfloat16)
    scales = []
    norms = []
    for t in range(step_count - 2, -1, -1):
        whole = lax.all_gather(weighted, "state", axis=1, tiled=True)
        backward, weighted, scale_sum, norm_part = backward_step(
            whole, transition_t, emitted_early[t], forward_probs[:, t, :]
        )
        vector_mat = lax.dynamic_update_slice(vector_mat, whole, (t * seq_count, 0))
        scales.append(scale_sum)
        backs.append(backward)
        norms.append(norm_part)
    backs = backs[::-1]
    scales = jnp.concatenate(scales[::-1], axis=1)
    partial_norms = jnp.concatenate(norms[::-1], axis=1)
    backward_probs = jnp.stack(backs, axis=1)
    norm_parts = lax.all_gather(partial_norms, "state", axis=0, tiled=False)
    norm_sums = jnp.sum(norm_parts, axis=0)
    denom = scales * norm_sums
    share_t = (forward_probs[:, :last, :] / denom[:, :, None]).astype(jnp.bfloat16)
    share_mat = jnp.transpose(share_t, (1, 0, 2)).reshape(last * seq_count, state_rows)
    moments = lax.dot_general(
        share_mat, vector_mat, (((0,), (0,)), ((), ())), preferred_element_type=jnp.float32
    )
    factor = float(states) * float(states) / float(seq_count * (step_count - 1))
    trans_counts = transition.astype(jnp.float32) * moments * factor
    return (backward_probs, trans_counts)


def solution(mesh):
    placed = (P("groups", None, "state"), P("groups", None), P("state", None), P("state", None))
    return jax.shard_map(
        on_device,
        mesh=mesh,
        in_specs=placed,
        out_specs=(P("groups", None, "state"), P(("groups", "state"), None)),
        check_vma=False,
    )
```

```python
import functools

import jax
import jax.numpy as jnp
from jax import lax
from jax.experimental import pallas as pl
from jax.experimental.pallas import tpu as pltpu
from jax.sharding import PartitionSpec as P

NT = (((1,), (1,)), ((), ()))


def _emit_kernel(ids_ref, em_ref, out_ref):
    k = pl.program_id(0)
    tv = em_ref.shape[1]

    @pl.when(k == 0)
    def _():
        out_ref[...] = jnp.zeros_like(out_ref)

    cols = lax.broadcasted_iota(jnp.int32, (ids_ref.shape[0], tv), 1) + k * tv
    onehot = (ids_ref[...] == cols).astype(em_ref.dtype)
    out_ref[...] += lax.dot_general(onehot, em_ref[...], NT, preferred_element_type=jnp.float32)


def emitted_rows(ids, emission, tv=1024):
    n = ids.shape[0]
    rows, vocab = emission.shape
    return pl.pallas_call(
        _emit_kernel,
        grid=(vocab // tv,),
        in_specs=[
            pl.BlockSpec((n, 1), lambda k: (0, 0)),
            pl.BlockSpec((rows, tv), lambda k: (0, k)),
        ],
        out_specs=pl.BlockSpec((n, rows), lambda k: (0, 0)),
        out_shape=jax.ShapeDtypeStruct((n, rows), jnp.float32),
        cost_estimate=pl.CostEstimate(
            flops=2 * n * rows * vocab, bytes_accessed=rows * vocab * 2 + n * rows * 4, transcendentals=0
        ),
    )(ids.reshape(n, 1), emission)


def _step_kernel(whole_ref, trans_ref, emit_ref, back_ref, wnext_ref, scale_ref, acc_ref, ssum_ref):
    k = pl.program_id(0)

    @pl.when(k == 0)
    def _():
        acc_ref[...] = jnp.zeros_like(acc_ref)
        ssum_ref[...] = jnp.zeros_like(ssum_ref)

    w = whole_ref[...]
    acc_ref[...] += jnp.dot(w, trans_ref[...], preferred_element_type=jnp.float32)
    ssum_ref[...] += jnp.sum(w.astype(jnp.float32), axis=1, keepdims=True)

    @pl.when(k == pl.num_programs(0) - 1)
    def _():
        s = ssum_ref[...]
        back = acc_ref[...] / s
        back_ref[...] = back
        wnext_ref[...] = (emit_ref[...] * back).astype(wnext_ref.dtype)
        scale_ref[...] = s


def backward_step(whole, transition_t, emit_next, tk=4096):
    b, states = whole.shape
    rows = transition_t.shape[1]
    full = lambda k: (0, 0)
    return pl.pallas_call(
        _step_kernel,
        grid=(states // tk,),
        in_specs=[
            pl.BlockSpec((b, tk), lambda k: (0, k)),
            pl.BlockSpec((tk, rows), lambda k: (k, 0)),
            pl.BlockSpec((b, rows), full),
        ],
        out_specs=[
            pl.BlockSpec((b, rows), full),
            pl.BlockSpec((b, rows), full),
            pl.BlockSpec((b, 1), full),
        ],
        out_shape=[
            jax.ShapeDtypeStruct((b, rows), jnp.float32),
            jax.ShapeDtypeStruct((b, rows), jnp.bfloat16),
            jax.ShapeDtypeStruct((b, 1), jnp.float32),
        ],
        scratch_shapes=[pltpu.VMEM((b, rows), jnp.float32), pltpu.VMEM((b, 1), jnp.float32)],
        cost_estimate=pl.CostEstimate(
            flops=2 * b * rows * states, bytes_accessed=rows * states * 2 + b * states * 2, transcendentals=0
        ),
    )(whole, transition_t, emit_next)


def _transpose_kernel(x_ref, o_ref):
    o_ref[...] = x_ref[...].T


def transposed(x, tile=512):
    rows, cols = x.shape
    return pl.pallas_call(
        _transpose_kernel,
        grid=(cols // tile,),
        in_specs=[pl.BlockSpec((rows, tile), lambda j: (0, j))],
        out_specs=pl.BlockSpec((tile, rows), lambda j: (j, 0)),
        out_shape=jax.ShapeDtypeStruct((cols, rows), x.dtype),
    )(x)


def emitted_rows_xla(ids, emission):
    vocab = emission.shape[1]
    onehot = (ids[:, None] == lax.broadcasted_iota(jnp.int32, (1, vocab), 1)).astype(emission.dtype)
    return lax.dot_general(onehot, emission, NT, preferred_element_type=jnp.float32)


def on_device(forward_probs, token_ids, transition, emission):
    state_rows = transition.shape[0]
    states = transition.shape[1]
    seq_count = token_ids.shape[0]
    step_count = token_ids.shape[1]
    last = step_count - 1
    emitted_last = emitted_rows_xla(token_ids[:, last], emission)
    early_ids = token_ids[:, :last].T.reshape(-1)
    emitted_early = emitted_rows(early_ids, emission).reshape(last, seq_count, state_rows)
    weighted = emitted_last.astype(jnp.bfloat16)
    transition_t = transposed(transition)
    backs = [jnp.ones((seq_count, state_rows), jnp.float32)]
    vector_mat = jnp.zeros((last * seq_count, states), jnp.bfloat16)
    scales = []
    norms = []
    for t in range(step_count - 2, -1, -1):
        whole = lax.all_gather(weighted, "state", axis=1, tiled=True)
        backward, weighted, scale_sum = backward_step(whole, transition_t, emitted_early[t])
        norm_part = jnp.sum(forward_probs[:, t, :] * backward, axis=1, keepdims=True)
        vector_mat = lax.dynamic_update_slice(vector_mat, whole, (t * seq_count, 0))
        scales.append(scale_sum)
        backs.append(backward)
        norms.append(norm_part)
    backs = backs[::-1]
    scales = jnp.concatenate(scales[::-1], axis=1)
    partial_norms = jnp.concatenate(norms[::-1], axis=1)
    backward_probs = jnp.stack(backs, axis=1)
    norm_parts = lax.all_gather(partial_norms, "state", axis=0, tiled=False)
    norm_sums = jnp.sum(norm_parts, axis=0)
    denom = scales * norm_sums
    share_t = (forward_probs[:, :last, :] / denom[:, :, None]).astype(jnp.bfloat16)
    share_mat = jnp.transpose(share_t, (1, 0, 2)).reshape(last * seq_count, state_rows)
    moments = lax.dot_general(
        share_mat, vector_mat, (((0,), (0,)), ((), ())), preferred_element_type=jnp.float32
    )
    factor = float(states) * float(states) / float(seq_count * (step_count - 1))
    trans_counts = transition.astype(jnp.float32) * moments * factor
    return (backward_probs, trans_counts)


def solution(mesh):
    placed = (P("groups", None, "state"), P("groups", None), P("state", None), P("state", None))
    return jax.shard_map(
        on_device,
        mesh=mesh,
        in_specs=placed,
        out_specs=(P("groups", None, "state"), P(("groups", "state"), None)),
        check_vma=False,
    )
```

```python
import functools

import jax
import jax.numpy as jnp
from jax import lax
from jax.experimental import pallas as pl
from jax.experimental.pallas import tpu as pltpu
from jax.sharding import PartitionSpec as P

NT = (((1,), (1,)), ((), ()))


def _emit_kernel(ids_ref, em_ref, out_ref):
    k = pl.program_id(0)
    tv = em_ref.shape[1]

    @pl.when(k == 0)
    def _():
        out_ref[...] = jnp.zeros_like(out_ref)

    cols = lax.broadcasted_iota(jnp.int32, (ids_ref.shape[0], tv), 1) + k * tv
    onehot = (ids_ref[...] == cols).astype(em_ref.dtype)
    out_ref[...] += lax.dot_general(onehot, em_ref[...], NT, preferred_element_type=jnp.float32)


def emitted_rows(ids, emission, tv=1024):
    n = ids.shape[0]
    rows, vocab = emission.shape
    return pl.pallas_call(
        _emit_kernel,
        grid=(vocab // tv,),
        in_specs=[
            pl.BlockSpec((n, 1), lambda k: (0, 0)),
            pl.BlockSpec((rows, tv), lambda k: (0, k)),
        ],
        out_specs=pl.BlockSpec((n, rows), lambda k: (0, 0)),
        out_shape=jax.ShapeDtypeStruct((n, rows), jnp.float32),
        cost_estimate=pl.CostEstimate(
            flops=2 * n * rows * vocab, bytes_accessed=rows * vocab * 2 + n * rows * 4, transcendentals=0
        ),
    )(ids.reshape(n, 1), emission)


def _step_kernel(whole_ref, trans_ref, emit_ref, fwd_ref, back_ref, wnext_ref, scale_ref, norm_ref, acc_ref, ssum_ref):
    k = pl.program_id(0)

    @pl.when(k == 0)
    def _():
        acc_ref[...] = jnp.zeros_like(acc_ref)
        ssum_ref[...] = jnp.zeros_like(ssum_ref)

    w = whole_ref[...]
    acc_ref[...] += jnp.dot(w, trans_ref[...], preferred_element_type=jnp.float32)
    ssum_ref[...] += jnp.sum(w.astype(jnp.float32), axis=1, keepdims=True)

    @pl.when(k == pl.num_programs(0) - 1)
    def _():
        s = ssum_ref[...]
        back = acc_ref[...] / s
        back_ref[...] = back
        wnext_ref[...] = (emit_ref[...] * back).astype(wnext_ref.dtype)
        scale_ref[...] = s
        norm_ref[...] = jnp.sum(fwd_ref[...] * back, axis=1, keepdims=True)


def backward_step(whole, transition_t, emit_next, fwd, tk=4096):
    b, states = whole.shape
    rows = transition_t.shape[1]
    full = lambda k: (0, 0)
    return pl.pallas_call(
        _step_kernel,
        grid=(states // tk,),
        in_specs=[
            pl.BlockSpec((b, tk), lambda k: (0, k)),
            pl.BlockSpec((tk, rows), lambda k: (k, 0)),
            pl.BlockSpec((b, rows), full),
            pl.BlockSpec((b, rows), full),
        ],
        out_specs=[
            pl.BlockSpec((b, rows), full),
            pl.BlockSpec((b, rows), full),
            pl.BlockSpec((b, 1), full),
            pl.BlockSpec((b, 1), full),
        ],
        out_shape=[
            jax.ShapeDtypeStruct((b, rows), jnp.float32),
            jax.ShapeDtypeStruct((b, rows), jnp.bfloat16),
            jax.ShapeDtypeStruct((b, 1), jnp.float32),
            jax.ShapeDtypeStruct((b, 1), jnp.float32),
        ],
        scratch_shapes=[pltpu.VMEM((b, rows), jnp.float32), pltpu.VMEM((b, 1), jnp.float32)],
        cost_estimate=pl.CostEstimate(
            flops=2 * b * rows * states, bytes_accessed=rows * states * 2 + b * states * 2, transcendentals=0
        ),
    )(whole, transition_t, emit_next, fwd)


def _transpose_kernel(x_ref, o_ref):
    o_ref[...] = x_ref[...].T


def transposed(x, tile=512):
    rows, cols = x.shape
    return pl.pallas_call(
        _transpose_kernel,
        grid=(cols // tile,),
        in_specs=[pl.BlockSpec((rows, tile), lambda j: (0, j))],
        out_specs=pl.BlockSpec((tile, rows), lambda j: (j, 0)),
        out_shape=jax.ShapeDtypeStruct((cols, rows), x.dtype),
    )(x)


def emitted_rows_xla(ids, emission):
    vocab = emission.shape[1]
    onehot_t = (lax.broadcasted_iota(jnp.int32, (vocab, 1), 0) == ids[None, :]).astype(emission.dtype)
    return jnp.dot(emission, onehot_t, preferred_element_type=jnp.float32).T


def on_device(forward_probs, token_ids, transition, emission):
    state_rows = transition.shape[0]
    states = transition.shape[1]
    seq_count = token_ids.shape[0]
    step_count = token_ids.shape[1]
    last = step_count - 1
    emitted_last = emitted_rows_xla(token_ids[:, last], emission)
    early_ids = token_ids[:, :last].T.reshape(-1)
    emitted_early = emitted_rows(early_ids, emission).reshape(last, seq_count, state_rows)
    weighted = emitted_last.astype(jnp.bfloat16)
    transition_t = transposed(transition)
    backs = [jnp.ones((seq_count, state_rows), jnp.float32)]
    vector_mat = jnp.zeros((last * seq_count, states), jnp.bfloat16)
    scales = []
    norms = []
    for t in range(step_count - 2, -1, -1):
        whole = lax.all_gather(weighted, "state", axis=1, tiled=True)
        backward, weighted, scale_sum, norm_part = backward_step(
            whole, transition_t, emitted_early[t], forward_probs[:, t, :]
        )
        vector_mat = lax.dynamic_update_slice(vector_mat, whole, (t * seq_count, 0))
        scales.append(scale_sum)
        backs.append(backward)
        norms.append(norm_part)
    backs = backs[::-1]
    scales = jnp.concatenate(scales[::-1], axis=1)
    partial_norms = jnp.concatenate(norms[::-1], axis=1)
    backward_probs = jnp.stack(backs, axis=1)
    norm_parts = lax.all_gather(partial_norms, "state", axis=0, tiled=False)
    norm_sums = jnp.sum(norm_parts, axis=0)
    denom = scales * norm_sums
    share_t = (forward_probs[:, :last, :] / denom[:, :, None]).astype(jnp.bfloat16)
    share_mat = jnp.transpose(share_t, (1, 0, 2)).reshape(last * seq_count, state_rows)
    moments = lax.dot_general(
        share_mat, vector_mat, (((0,), (0,)), ((), ())), preferred_element_type=jnp.float32
    )
    factor = float(states) * float(states) / float(seq_count * (step_count - 1))
    trans_counts = transition.astype(jnp.float32) * moments * factor
    return (backward_probs, trans_counts)


def solution(mesh):
    placed = (P("groups", None, "state"), P("groups", None), P("state", None), P("state", None))
    return jax.shard_map(
        on_device,
        mesh=mesh,
        in_specs=placed,
        out_specs=(P("groups", None, "state"), P(("groups", "state"), None)),
        check_vma=False,
    )
```
